128 devices in a mesh: dp: 8 (over z, core), expert: 16 (over x, y).
Axes of the slice: x: 4, y: 4, z: 4, core: 2. Of those that a mesh axis runs over, the one named last changes fastest.
Arguments:
- residual_in: bfloat16 [8192, 2048], P(('dp', 'expert')), may hold values from -40 to 40
- attention_gain: float32 [2048], replicated, may hold values from 0.25 to 1.75
- query_weight: bfloat16 [2048, 2048], P(None, 'expert'), may hold values from -0.125 to 0.125
- key_weight: bfloat16 [2048, 2048], P(None, 'expert'), may hold values from -0.125 to 0.125
- value_weight: bfloat16 [2048, 2048], P(None, 'expert'), may hold values from -0.125 to 0.125
- output_weight: bfloat16 [2048, 2048], P('expert'), may hold values from -0.125 to 0.125
- prompt_keys: bfloat16 [24, 2048, 2048], P('dp', None, 'expert'), may hold values from -220 to 220
- prompt_values: bfloat16 [24, 2048, 2048], P('dp', None, 'expert'), may hold values from -12 to 12
- group_index: int32 [8, 32], P('dp'), may hold values from 0 to 2, never falling along the last dimension, each value on 1 to 16 neighbouring positions
- prompt_length: int32 [24], P('dp'), may hold values from 1 to 2048, 24576 in all
- own_length: int32 [256], P('dp'), may hold values from 1 to 32
- expert_gain: float32 [2048], replicated, may hold values from 0.25 to 1.75
- expert_ids: int32 [8192, 8], P(('dp', 'expert')), may hold values from 0 to 63, all different within a row; in each aligned block of 64 rows (0 to 63, 64 to 127, ...) at most 12 rows name the same one
- expert_mix: float32 [8192, 8], P(('dp', 'expert')), may hold values from 0.02 to 0.3
- gate_weight: bfloat16 [128, 2048, 512], P(('dp', 'expert')), may hold values from -0.125 to 0.125
- up_weight: bfloat16 [128, 2048, 512], P(('dp', 'expert')), may hold values from -0.125 to 0.125
- down_weight: bfloat16 [128, 512, 2048], P(('dp', 'expert')), may hold values from -0.1875 to 0.1875
Outputs:
- attention_update: bfloat16 [8192, 2048], P(('dp', 'expert'))
- expert_update: bfloat16 [8192, 2048], P(('dp', 'expert'))
The draws below stay inside these ranges and needn't reach their ends.
Inputs may be any that keep to these rules, and one draw needn't show every extreme that they name: `group_index`: each row holds the 32 requests of one index of dp; a group's requests are consecutive, every group has 1 to 16 requests and some group exactly 16. `prompt_length`: some prompt is exactly 2048 long. `expert_ids`: a token's 8 experts differ; among the 64 rows of one device no expert is named more than 12 times, a bound that some block reaches.
All inputs are finite; a program needn't handle non-finite values. No bound on the sum of `prompt_length` on one device may be relied on, other than what follows from the above.
Results may differ from the reference program's by a relative error of at most 0.025.
The reference program's roundings to bfloat16 on the way (of `normed`, `queries`, `weights`, `attended`, `expert_input`, `hidden` and `part`) count: a program that leaves them out, or rounds other values in their place, can miss the bound.
Values may be sent and summed in bfloat16 or wider, within the bound.
No kernel may reach another device: no remote copies, remote signals or barrier semaphores. Data moves between devices by JAX's collectives and lax.ppermute only.
A program may use at most 128 MiB of HBM per device.

```python
import math
import jax
import jax.numpy as jnp
import numpy as np
from jax import lax

D = 2048
H = 16
HD = 128
FF = 1024
TOP = 8
EXPERTS = 64
HSPLIT = 2
FF_DEV = 512
SHARDS = 128
REQ_DEV = 32
G_DEV = 3
GSIZE = 16
SB = 32
PMAX = 2048
REQUESTS = 256
GROUPS = 24
TOKENS = 8192
TOK_DEV = 64
CAP = 12
N_DP = 8
N_EXPERT = 16


def draw_residual_in(key, part):
    first, second = jax.random.split(key, 2)
    columns = jnp.exp(jax.random.uniform(second, (1, D), jnp.float32, math.log(0.5), math.log(5.0)))
    values = jnp.clip(jax.random.normal(first, (TOKENS, D), jnp.float32), -4.0, 4.0) * columns
    return values.astype(jnp.bfloat16)


def draw_prompt_keys(key, part):
    first = jax.random.fold_in(key, 0)
    values = jnp.clip(jax.random.normal(first, (GROUPS, PMAX, H * HD), jnp.float32), -4.0, 4.0)
    return values.astype(jnp.bfloat16)


def place_ends(values, rng, smallest, top_value):
    longest = values.shape.index(max(values.shape))
    spots = []
    for shift in (0, 1):
        where = [jax.random.randint(jax.random.fold_in(rng, axis), (), 0, length) for axis, length in enumerate(values.shape)]
        where[longest] = (where[longest] + shift) % values.shape[longest]
        spots.append(tuple(where))
    return values.at[spots[0]].set(smallest).at[spots[1]].set(top_value)


def shard_levels(rng, dims, pieces, smallest, high):
    loudness = 1.0
    for position, shards_of in pieces:
        steps = jax.random.uniform(jax.random.fold_in(jax.random.fold_in(rng, 6), position), (shards_of,), jnp.float32, smallest / len(pieces), high / len(pieces))
        loudness = loudness * jnp.repeat(jnp.exp(steps), dims[position] // shards_of).reshape((-1,) + (1,) * (len(dims) - 1 - position))
    return loudness


def split_up(number_of, total, most, slope):
    portions = [(1 << 20) // math.isqrt(rank ** slope) + 1 for rank in range(2, number_of + 1)]
    spare, given = total - most - (number_of - 1), [1] * (number_of - 1)
    while spare > 0:
        candidates = [i for i in range(number_of - 1) if given[i] < most]
        whole, left = sum([portions[i] for i in candidates]), spare
        for i in candidates:
            more = min(most - given[i], max(1, left * portions[i] // whole), spare)
            given[i] = given[i] + more
            spare = spare - more
    return np.array([most] + given)


def uneven(rng, number_of, total, most, slope):
    if number_of == 2:
        one = jax.random.randint(rng, (), max(1, total - most), min(most, total - 1) + 1)
        return jnp.stack([one, total - one])
    tallies = jnp.asarray(split_up(number_of, total, most, slope), jnp.int32)
    twos = (number_of - 1) // 2
    giver, receiver = tallies[1:1 + 2 * twos:2], tallies[2:2 + 2 * twos:2]
    room = jnp.minimum(giver - 1, most - receiver)
    shifted = jax.random.randint(jax.random.fold_in(rng, 1), (twos,), 0, 1 << 20) % (room + 1)
    tallies = tallies.at[1:1 + 2 * twos:2].set(giver - shifted).at[2:2 + 2 * twos:2].set(receiver + shifted)
    return tallies[jax.random.permutation(jax.random.fold_in(rng, 2), number_of)]


def assign_block(rng, own, number, rows, amount, top, reach, lean):
    ranking = jax.random.permutation(rng, amount)
    packed, usual = portions_of(amount, rows * top, reach, lean, True), portions_of(amount, rows * top, reach, lean, False)
    places = jnp.arange(amount)

    def named(tallies, offset_by):
        used = int((tallies > 0).sum())
        fixed = max(1, used // 4)
        passed = fixed + (places - fixed + offset_by * (used - fixed)) % max(1, amount - fixed)
        return jnp.zeros((amount,), jnp.int32).at[ranking[jnp.where(places < fixed, places, passed)]].set(jnp.asarray(tallies, jnp.int32))

    tallies = jnp.where(number % 4 == 0, named(packed, number // 4), named(usual, number - number // 4 - 1))
    mixed = jax.random.permutation(jax.random.fold_in(own, 3), amount)
    donor, receiver = mixed[0:amount // 2 * 2:2], mixed[1:amount // 2 * 2:2]
    slack = jnp.minimum(tallies[donor] - 1, reach - tallies[receiver]) // 2
    slack = jnp.where((donor == ranking[0]) | (receiver == ranking[0]) | (tallies[receiver] == 0), 0, jnp.maximum(slack, 0))
    passed = jax.random.randint(jax.random.fold_in(own, 4), (amount // 2,), 0, 1 << 20) % (slack + 1)
    tallies = tallies.at[donor].add(-passed).at[receiver].add(passed)
    labels = jnp.searchsorted(jnp.cumsum(tallies), jnp.arange(rows * top), side="right").astype(jnp.int32)
    listing = labels.reshape(top, rows).T
    listing = listing[jax.random.permutation(jax.random.fold_in(own, 1), rows)]
    offset_by = jax.random.randint(jax.random.fold_in(own, 2), (rows, 1), 0, top)
    return jnp.take_along_axis(listing, (jnp.arange(top)[None, :] + offset_by) % top, axis=1)


def portions_of(amount, total, bound, skew, full):
    weights = [(1 << 20) // math.isqrt(rank ** skew) + 1 for rank in range(1, amount + 1)]
    largest = bound if full else min(bound, max(-(-total // amount), total * weights[0] // sum(weights)))
    least = 1 if total - largest >= amount - 1 else 0
    holding, spare = [largest] + [least] * (amount - 1), total - largest - least * (amount - 1)
    while spare > 0:
        movable = [i for i in range(1, amount) if holding[i] < largest] or [i for i in range(1, amount) if holding[i] < bound]
        pool, left = sum([weights[i] for i in movable]), spare
        for i in movable:
            addition = min(bound - holding[i], max(1, left * weights[i] // pool), spare)
            holding[i] = holding[i] + addition
            spare = spare - addition
    return np.array(holding)


def bell_draw(own_key, extent, scale, most, cuts=(), kind=jnp.bfloat16):
    drawn = scale * jax.random.normal(own_key, extent, jnp.float32)
    if cuts:
        drawn = drawn * shard_levels(own_key, extent, cuts, -0.22, 0.18)
    return jnp.clip(drawn, -most, most).astype(kind)


def setup_inputs(seed: int = 0) -> dict:
    splits = jax.random.split(jax.random.key(seed), 18)
    residual_in = draw_residual_in(jax.random.fold_in(splits[17], 71), 0)
    attention_gain = jnp.clip(1.0 + 0.15 * jax.random.normal(splits[1], (D,), jnp.float32), 0.25, 1.75)
    query_weight = bell_draw(splits[2], (D, H * HD), D ** -0.5, 0.125, ((1, 16),))
    key_weight = bell_draw(splits[3], (D, H * HD), D ** -0.5, 0.125, ((1, 16),))
    value_weight = bell_draw(splits[4], (D, H * HD), D ** -0.5, 0.125, ((1, 16),))
    output_weight = bell_draw(splits[5], (H * HD, D), (H * HD) ** -0.5, 0.125, ((0, 16),))
    prompt_keys = draw_prompt_keys(jax.random.fold_in(splits[17], 71), 0)
    prompt_values = bell_draw(splits[7], (GROUPS, PMAX, H * HD), 2.0, 12.0, ((0, 8), (2, 16)))
    group_index = jax.vmap(lambda own: jnp.searchsorted(jnp.cumsum(uneven(own, G_DEV, REQ_DEV, GSIZE, 1)), jnp.arange(REQ_DEV), side="right"))(jax.random.split(splits[8], N_DP)).reshape((N_DP, REQ_DEV)).astype(jnp.int32)
    prompt_length = uneven(splits[9], GROUPS, GROUPS * PMAX // 2, PMAX, 1).astype(jnp.int32)
    own_length = place_ends(jax.random.randint(splits[10], (REQUESTS,), 1, SB + 1), jax.random.fold_in(splits[10], 1), 1, SB).astype(jnp.int32)
    expert_gain = jnp.clip(1.0 + 0.15 * jax.random.normal(splits[11], (D,), jnp.float32), 0.25, 1.75)
    expert_ids_keys = jax.random.split(jax.random.fold_in(splits[12], 1), TOKENS // TOK_DEV)
    expert_ids_turns = jax.random.permutation(jax.random.fold_in(splits[12], 3), TOKENS // TOK_DEV)
    expert_ids = jax.vmap(lambda own, number: assign_block(jax.random.fold_in(splits[12], 2), own, number, TOK_DEV, EXPERTS, TOP, CAP, 2))(expert_ids_keys, expert_ids_turns).reshape((TOKENS, TOP))
    expert_mix = jnp.clip(0.02 + 0.28 * jax.random.uniform(splits[13], (TOKENS, TOP), jnp.float32) ** shard_levels(splits[13], (TOKENS, TOP), ((0, 128),), -0.2, 0.2), 0.02, 0.3)
    gate_weight = bell_draw(splits[14], (SHARDS, D, FF_DEV), D ** -0.5, 0.125, ((0, 128),))
    up_weight = bell_draw(splits[15], (SHARDS, D, FF_DEV), D ** -0.5, 0.125, ((0, 128),))
    down_weight = bell_draw(splits[16], (SHARDS, FF_DEV, D), FF ** -0.5, 0.1875, ((0, 128),))
    return {"residual_in": residual_in, "attention_gain": attention_gain, "query_weight": query_weight, "key_weight": key_weight, "value_weight": value_weight, "output_weight": output_weight, "prompt_keys": prompt_keys, "prompt_values": prompt_values, "group_index": group_index, "prompt_length": prompt_length, "own_length": own_length, "expert_gain": expert_gain, "expert_ids": expert_ids, "expert_mix": expert_mix, "gate_weight": gate_weight, "up_weight": up_weight, "down_weight": down_weight}


epsilon = 1e-06

def rms_scale(values, gain):
    widened = values.astype(jnp.float32)
    spread = lax.optimization_barrier(jnp.mean(widened * widened, axis=-1, keepdims=True))
    return (widened * lax.rsqrt(spread + epsilon) * gain).astype(jnp.bfloat16)

def widen_rounded(values):
    return lax.optimization_barrier(values.astype(jnp.bfloat16)).astype(jnp.float32)

def attend(queries, new_keys, new_values, prompt_keys, prompt_values, group_index, prompt_length, own_length):
    layout = (REQUESTS, SB, H, HD)
    owners = jnp.arange(REQUESTS, dtype=jnp.int32) // REQ_DEV * G_DEV + group_index.reshape(-1).astype(jnp.int32)
    scale = HD ** (-0.5)
    prompt_positions = jnp.arange(PMAX, dtype=jnp.int32)
    positions = jnp.arange(SB, dtype=jnp.int32)

    def one_request(item):
        query_rows, key_rows, value_rows, owner, count = item
        group_keys = lax.dynamic_index_in_dim(prompt_keys, owner, 0, keepdims=False).reshape(PMAX, H, HD).astype(jnp.float32)
        group_values = lax.dynamic_index_in_dim(prompt_values, owner, 0, keepdims=False).reshape(PMAX, H, HD).astype(jnp.float32)
        limit = lax.dynamic_index_in_dim(prompt_length, owner, 0, keepdims=False)
        widened = query_rows.astype(jnp.float32)
        scores = jnp.einsum('ihd,jhd->hij', widened, group_keys) * scale
        scores = jnp.where(prompt_positions[None, None, :] < limit, scores, -jnp.inf)
        own_scores = jnp.einsum('ihd,jhd->hij', widened, key_rows.astype(jnp.float32)) * scale
        own_scores = jnp.where(positions[None, None, :] < count, own_scores, -jnp.inf)
        highest = jnp.maximum(lax.optimization_barrier(jnp.max(scores, axis=-1)), lax.optimization_barrier(jnp.max(own_scores, axis=-1)))
        prompt_weights = widen_rounded(jnp.exp(scores - highest[..., None]))
        own_weights = widen_rounded(jnp.exp(own_scores - highest[..., None]))
        summed = jnp.einsum('hij,jhd->ihd', prompt_weights, group_values)
        summed = summed + jnp.einsum('hij,jhd->ihd', own_weights, value_rows.astype(jnp.float32))
        totals = lax.optimization_barrier(jnp.sum(prompt_weights, axis=-1)) + lax.optimization_barrier(jnp.sum(own_weights, axis=-1))
        result = summed / jnp.transpose(totals)[..., None]
        return result.astype(jnp.bfloat16).reshape(SB, H * HD)
    items = (queries.reshape(layout), new_keys.reshape(layout), new_values.reshape(layout), owners, own_length.astype(jnp.int32))
    return lax.map(one_request, items).reshape(TOKENS, H * HD)

def experts_layer(expert_input, expert_ids, expert_mix, gate_weight, up_weight, down_weight):
    chosen = expert_ids.reshape(-1).astype(jnp.int32)
    routes = chosen.shape[0]
    owners = jnp.arange(routes, dtype=jnp.int32) // TOP
    matches = (chosen[:, None] == jnp.arange(EXPERTS, dtype=jnp.int32)[None, :]).astype(jnp.int32)
    slots = lax.optimization_barrier(jnp.sum((jnp.cumsum(matches, axis=0) - matches) * matches, axis=1)).astype(jnp.int32)
    capacity_all = N_DP * N_EXPERT * CAP
    table = jnp.full((EXPERTS, capacity_all), TOKENS, jnp.int32).at[chosen, slots].set(owners)
    shares = jnp.zeros((EXPERTS, capacity_all), jnp.float32).at[chosen, slots].set(expert_mix.reshape(-1))
    padded = jnp.concatenate([expert_input, jnp.zeros((1, D), jnp.bfloat16)], axis=0)

    def one_expert(total, expert):
        picked = table[expert]
        rows = padded[picked]
        summed = jnp.zeros((capacity_all, D), jnp.float32)
        for half in range(HSPLIT):
            shard = expert * HSPLIT + half
            gated = jnp.dot(rows, gate_weight[shard], preferred_element_type=jnp.float32)
            lifted = jnp.dot(rows, up_weight[shard], preferred_element_type=jnp.float32)
            hidden = (jax.nn.silu(gated) * lifted).astype(jnp.bfloat16)
            summed = summed + widen_rounded(jnp.dot(hidden, down_weight[shard], preferred_element_type=jnp.float32))
        total = total.at[picked].add(shares[expert][:, None] * summed, mode='drop')
        return (total, None)
    total = lax.scan(one_expert, jnp.zeros((TOKENS, D), jnp.float32), jnp.arange(EXPERTS, dtype=jnp.int32))[0]
    return total.astype(jnp.bfloat16)

def reference(residual_in, attention_gain, query_weight, key_weight, value_weight, output_weight, prompt_keys, prompt_values, group_index, prompt_length, own_length, expert_gain, expert_ids, expert_mix, gate_weight, up_weight, down_weight):
    normed = rms_scale(residual_in, attention_gain)
    queries = jnp.dot(normed, query_weight, preferred_element_type=jnp.float32).astype(jnp.bfloat16)
    new_keys = jnp.dot(normed, key_weight, preferred_element_type=jnp.float32).astype(jnp.bfloat16)
    new_values = jnp.dot(normed, value_weight, preferred_element_type=jnp.float32).astype(jnp.bfloat16)
    attended = attend(queries, new_keys, new_values, prompt_keys, prompt_values, group_index, prompt_length, own_length)
    attention_update = jnp.dot(attended, output_weight, preferred_element_type=jnp.float32).astype(jnp.bfloat16)
    expert_input = rms_scale(residual_in.astype(jnp.float32) + attention_update.astype(jnp.float32), expert_gain)
    expert_update = experts_layer(expert_input, expert_ids, expert_mix, gate_weight, up_weight, down_weight)
    return (attention_update, expert_update)
```

```python
import jax
import jax.numpy as jnp
from jax import lax
from jax.sharding import PartitionSpec as P

HD = 128
FF = 1024
TOP = 8
GSIZE = 16
SB = 32


epsilon = 1e-06


def rms_scale(values, gain):
    widened = values.astype(jnp.float32)
    spread = jnp.mean(widened * widened, axis=-1, keepdims=True)
    return (widened * lax.rsqrt(spread + epsilon) * gain).astype(jnp.bfloat16)


def expert_block(block, gate_weight, up_weight, down_weight):
    shape_kept = block.shape
    flat = block.reshape(-1, shape_kept[-1])
    gated = jnp.dot(flat, gate_weight[0], preferred_element_type=jnp.float32)
    lifted = jnp.dot(flat, up_weight[0], preferred_element_type=jnp.float32)
    hidden = (jax.nn.silu(gated) * lifted).astype(jnp.bfloat16)
    produced = jnp.dot(hidden, down_weight[0], preferred_element_type=jnp.float32).astype(
        jnp.bfloat16
    )
    return produced.reshape(shape_kept)


def per_device(
    residual_in,
    attention_gain,
    query_weight,
    key_weight,
    value_weight,
    output_weight,
    prompt_keys,
    prompt_values,
    group_index,
    prompt_length,
    own_length,
    expert_gain,
    expert_ids,
    expert_mix,
    gate_weight,
    up_weight,
    down_weight,
):
    tok_rows, width = residual_in.shape
    local_width = query_weight.shape[1]
    heads_here = local_width // HD
    requests = group_index.shape[1]
    longest = prompt_keys.shape[1]
    groups_here = prompt_keys.shape[0]
    normed = rms_scale(residual_in, attention_gain)
    piece = lax.all_gather(normed, "expert", axis=0, tiled=True)
    query_part = jnp.dot(piece, query_weight, preferred_element_type=jnp.float32).astype(
        jnp.bfloat16
    )
    key_part = jnp.dot(piece, key_weight, preferred_element_type=jnp.float32).astype(jnp.bfloat16)
    value_part = jnp.dot(piece, value_weight, preferred_element_type=jnp.float32).astype(
        jnp.bfloat16
    )
    projected = jnp.concatenate([query_part, key_part, value_part], axis=1)
    layout = (requests, SB, heads_here, HD)
    queries = projected[:, :local_width].reshape(layout)
    new_keys = projected[:, local_width : 2 * local_width].reshape(layout)
    new_values = projected[:, 2 * local_width :].reshape(layout)
    scale = HD ** (-0.5)
    positions = jnp.arange(SB, dtype=jnp.int32)
    own_scores = (
        jnp.einsum("rihd,rjhd->rhij", queries, new_keys, preferred_element_type=jnp.float32) * scale
    )
    own_scores = jnp.where(
        positions[None, None, None, :] < own_length[:, None, None, None], own_scores, -jnp.inf
    )
    member = group_index[0]
    prompt_positions = jnp.arange(longest, dtype=jnp.int32)

    def group_step(group, attended):
        first = jnp.sum((member < group).astype(jnp.int32))
        start = jnp.minimum(first, requests - GSIZE)
        window_queries = lax.dynamic_slice_in_dim(queries, start, GSIZE, 0)
        group_keys = lax.dynamic_index_in_dim(prompt_keys, group, 0, keepdims=False).reshape(
            longest, heads_here, HD
        )
        group_values = lax.dynamic_index_in_dim(prompt_values, group, 0, keepdims=False).reshape(
            longest, heads_here, HD
        )
        scores = (
            jnp.einsum(
                "rihd,jhd->rhij", window_queries, group_keys, preferred_element_type=jnp.float32
            )
            * scale
        )
        limit = lax.dynamic_index_in_dim(prompt_length, group, 0, keepdims=False)
        scores = jnp.where(prompt_positions < limit, scores, -jnp.inf)
        window_own = lax.dynamic_slice_in_dim(own_scores, start, GSIZE, 0)
        highest = jnp.maximum(jnp.max(scores, axis=-1), jnp.max(window_own, axis=-1))
        prompt_weights = jnp.exp(scores - highest[..., None]).astype(jnp.bfloat16)
        own_weights = jnp.exp(window_own - highest[..., None]).astype(jnp.bfloat16)
        window_values = lax.dynamic_slice_in_dim(new_values, start, GSIZE, 0)
        summed = jnp.einsum(
            "rhij,jhd->rihd", prompt_weights, group_values, preferred_element_type=jnp.float32
        )
        summed = summed + jnp.einsum(
            "rhij,rjhd->rihd", own_weights, window_values, preferred_element_type=jnp.float32
        )
        totals = jnp.sum(prompt_weights, axis=-1, dtype=jnp.float32) + jnp.sum(
            own_weights, axis=-1, dtype=jnp.float32
        )
        result = (summed / jnp.transpose(totals, (0, 2, 1))[..., None]).astype(jnp.bfloat16)
        inside = lax.dynamic_slice_in_dim(member, start, GSIZE, 0) == group
        current = lax.dynamic_slice_in_dim(attended, start, GSIZE, 0)
        merged = jnp.where(inside[:, None, None, None], result, current)
        return lax.dynamic_update_slice_in_dim(attended, merged, start, 0)

    attended = lax.fori_loop(0, groups_here, group_step, jnp.zeros(layout, jnp.bfloat16))
    flat_attended = attended.reshape(requests * SB, local_width)
    piece = flat_attended
    expert_groups = lax.axis_size("expert")
    projected_out = jnp.dot(piece, output_weight, preferred_element_type=jnp.float32).astype(jnp.bfloat16)
    partials = lax.all_to_all(
        projected_out.reshape(expert_groups, tok_rows, width), "expert", 0, 0, tiled=True
    )
    attention_update = jnp.sum(partials.astype(jnp.float32), axis=0).astype(jnp.bfloat16)
    expert_input = rms_scale(
        residual_in.astype(jnp.float32) + attention_update.astype(jnp.float32), expert_gain
    )
    data_groups = lax.axis_size("dp")
    devices = data_groups * expert_groups
    hidden_split = FF // gate_weight.shape[2]
    experts = devices // hidden_split
    capacity = max(2, tok_rows * TOP * 3 // (2 * experts))
    chosen = expert_ids.reshape(-1)
    routes_here = chosen.shape[0]
    owners = jnp.arange(routes_here, dtype=jnp.int32) // TOP
    matches = (chosen[:, None] == jnp.arange(experts, dtype=jnp.int32)[None, :]).astype(jnp.int32)
    slots = jnp.sum((jnp.cumsum(matches, axis=0) - matches) * matches, axis=1)
    table = (
        jnp.full((experts * capacity,), tok_rows, jnp.int32)
        .at[chosen * capacity + slots]
        .set(owners)
    )
    lanes = 128
    sub = width // lanes
    tiles = expert_input.reshape(tok_rows, sub, lanes)
    padded = jnp.concatenate([tiles, jnp.zeros((1, sub, lanes), jnp.bfloat16)], axis=0)
    index = jnp.broadcast_to(
        table.reshape(experts, 1, capacity), (experts, hidden_split, capacity)
    ).reshape(-1)
    outgoing = padded[index].reshape(devices, capacity * sub, lanes)
    arrived = lax.all_to_all(outgoing, ("dp", "expert"), 0, 0, tiled=True)
    produced = expert_block(
        arrived.reshape(devices * capacity, width), gate_weight, up_weight, down_weight
    )
    returned = lax.all_to_all(
        produced.reshape(devices, capacity * sub, lanes), ("dp", "expert"), 0, 0, tiled=True
    )
    pieces = returned.reshape(experts, hidden_split, capacity, sub, lanes)[chosen, :, slots]
    blended = jnp.sum(pieces.astype(jnp.float32), axis=1) * expert_mix.reshape(-1)[:, None, None]
    expert_update = (
        jnp.sum(blended.reshape(tok_rows, TOP, sub, lanes), axis=1)
        .reshape(tok_rows, width)
        .astype(jnp.bfloat16)
    )
    return (attention_update, expert_update)


def solution(mesh):
    in_specs = (
        P(("dp", "expert"), None),
        P(),
        P(None, "expert"),
        P(None, "expert"),
        P(None, "expert"),
        P("expert", None),
        P("dp", None, "expert"),
        P("dp", None, "expert"),
        P("dp", None),
        P("dp"),
        P("dp"),
        P(),
        P(("dp", "expert"), None),
        P(("dp", "expert"), None),
        P(("dp", "expert"), None, None),
        P(("dp", "expert"), None, None),
        P(("dp", "expert"), None, None),
    )
    out_specs = (P(("dp", "expert"), None), P(("dp", "expert"), None))
    return jax.shard_map(
        per_device, mesh=mesh, in_specs=in_specs, out_specs=out_specs, check_vma=False
    )
```

```python
import jax
import jax.numpy as jnp
from jax import lax
from jax.sharding import PartitionSpec as P

HD = 128
FF = 1024
TOP = 8
GSIZE = 16
SB = 32


epsilon = 1e-06


def rms_scale(values, gain):
    widened = values.astype(jnp.float32)
    spread = jnp.mean(widened * widened, axis=-1, keepdims=True)
    return (widened * lax.rsqrt(spread + epsilon) * gain).astype(jnp.bfloat16)


def expert_block(block, gate_weight, up_weight, down_weight):
    rows, sub, lanes = block.shape
    gate = gate_weight[0].reshape(sub, lanes, -1)
    up = up_weight[0].reshape(sub, lanes, -1)
    down = down_weight[0].reshape(-1, sub, lanes)
    contract = (((1, 2), (0, 1)), ((), ()))
    gated = lax.dot_general(block, gate, contract, preferred_element_type=jnp.float32)
    lifted = lax.dot_general(block, up, contract, preferred_element_type=jnp.float32)
    hidden = (jax.nn.silu(gated) * lifted).astype(jnp.bfloat16)
    return lax.dot_general(
        hidden, down, (((1,), (0,)), ((), ())), preferred_element_type=jnp.float32
    ).astype(jnp.bfloat16)


def per_device(
    residual_in,
    attention_gain,
    query_weight,
    key_weight,
    value_weight,
    output_weight,
    prompt_keys,
    prompt_values,
    group_index,
    prompt_length,
    own_length,
    expert_gain,
    expert_ids,
    expert_mix,
    gate_weight,
    up_weight,
    down_weight,
):
    tok_rows, width = residual_in.shape
    local_width = query_weight.shape[1]
    heads_here = local_width // HD
    requests = group_index.shape[1]
    longest = prompt_keys.shape[1]
    groups_here = prompt_keys.shape[0]
    normed = rms_scale(residual_in, attention_gain)
    piece = lax.all_gather(normed, "expert", axis=0, tiled=True)
    query_part = jnp.dot(piece, query_weight, preferred_element_type=jnp.float32).astype(
        jnp.bfloat16
    )
    key_part = jnp.dot(piece, key_weight, preferred_element_type=jnp.float32).astype(jnp.bfloat16)
    value_part = jnp.dot(piece, value_weight, preferred_element_type=jnp.float32).astype(
        jnp.bfloat16
    )
    projected = jnp.concatenate([query_part, key_part, value_part], axis=1)
    layout = (requests, SB, heads_here, HD)
    queries = projected[:, :local_width].reshape(layout)
    new_keys = projected[:, local_width : 2 * local_width].reshape(layout)
    new_values = projected[:, 2 * local_width :].reshape(layout)
    scale = HD ** (-0.5)
    positions = jnp.arange(SB, dtype=jnp.int32)
    own_scores = (
        jnp.einsum("rihd,rjhd->rhij", queries, new_keys, preferred_element_type=jnp.float32) * scale
    )
    own_scores = jnp.where(
        positions[None, None, None, :] < own_length[:, None, None, None], own_scores, -jnp.inf
    )
    member = group_index[0]
    prompt_positions = jnp.arange(longest, dtype=jnp.int32)

    def group_step(group, attended):
        first = jnp.sum((member < group).astype(jnp.int32))
        start = jnp.minimum(first, requests - GSIZE)
        window_queries = lax.dynamic_slice_in_dim(queries, start, GSIZE, 0)
        group_keys = lax.dynamic_index_in_dim(prompt_keys, group, 0, keepdims=False).reshape(
            longest, heads_here, HD
        )
        group_values = lax.dynamic_index_in_dim(prompt_values, group, 0, keepdims=False).reshape(
            longest, heads_here, HD
        )
        scores = (
            jnp.einsum(
                "rihd,jhd->rhij", window_queries, group_keys, preferred_element_type=jnp.float32
            )
            * scale
        )
        limit = lax.dynamic_index_in_dim(prompt_length, group, 0, keepdims=False)
        scores = jnp.where(prompt_positions < limit, scores, -jnp.inf)
        window_own = lax.dynamic_slice_in_dim(own_scores, start, GSIZE, 0)
        highest = jnp.maximum(jnp.max(scores, axis=-1), jnp.max(window_own, axis=-1))
        prompt_weights = jnp.exp(scores - highest[..., None]).astype(jnp.bfloat16)
        own_weights = jnp.exp(window_own - highest[..., None]).astype(jnp.bfloat16)
        window_values = lax.dynamic_slice_in_dim(new_values, start, GSIZE, 0)
        summed = jnp.einsum(
            "rhij,jhd->rihd", prompt_weights, group_values, preferred_element_type=jnp.float32
        )
        summed = summed + jnp.einsum(
            "rhij,rjhd->rihd", own_weights, window_values, preferred_element_type=jnp.float32
        )
        totals = jnp.sum(prompt_weights, axis=-1, dtype=jnp.float32) + jnp.sum(
            own_weights, axis=-1, dtype=jnp.float32
        )
        result = (summed / jnp.transpose(totals, (0, 2, 1))[..., None]).astype(jnp.bfloat16)
        inside = lax.dynamic_slice_in_dim(member, start, GSIZE, 0) == group
        current = lax.dynamic_slice_in_dim(attended, start, GSIZE, 0)
        merged = jnp.where(inside[:, None, None, None], result, current)
        return lax.dynamic_update_slice_in_dim(attended, merged, start, 0)

    attended = lax.fori_loop(0, groups_here, group_step, jnp.zeros(layout, jnp.bfloat16))
    flat_attended = attended.reshape(requests * SB, local_width)
    piece = flat_attended
    expert_groups = lax.axis_size("expert")
    projected_out = jnp.dot(piece, output_weight, preferred_element_type=jnp.float32).astype(jnp.bfloat16)
    partials = lax.all_to_all(
        projected_out.reshape(expert_groups, tok_rows, width), "expert", 0, 0, tiled=True
    )
    attention_update = jnp.sum(partials.astype(jnp.float32), axis=0).astype(jnp.bfloat16)
    expert_input = rms_scale(
        residual_in.astype(jnp.float32) + attention_update.astype(jnp.float32), expert_gain
    )
    data_groups = lax.axis_size("dp")
    devices = data_groups * expert_groups
    hidden_split = FF // gate_weight.shape[2]
    experts = devices // hidden_split
    capacity = max(2, tok_rows * TOP * 3 // (2 * experts))
    chosen = expert_ids.reshape(-1)
    routes_here = chosen.shape[0]
    owners = jnp.arange(routes_here, dtype=jnp.int32) // TOP
    matches = (chosen[:, None] == jnp.arange(experts, dtype=jnp.int32)[None, :]).astype(jnp.int32)
    slots = jnp.sum((jnp.cumsum(matches, axis=0) - matches) * matches, axis=1)
    table = (
        jnp.full((experts * capacity,), tok_rows, jnp.int32)
        .at[chosen * capacity + slots]
        .set(owners)
    )
    lanes = 128
    sub = width // lanes
    tiles = expert_input.reshape(tok_rows, sub, lanes)
    padded = jnp.concatenate([tiles, jnp.zeros((1, sub, lanes), jnp.bfloat16)], axis=0)
    index = jnp.broadcast_to(
        table.reshape(experts, 1, capacity), (experts, hidden_split, capacity)
    ).reshape(-1)
    outgoing = padded[index].reshape(devices, capacity * sub, lanes)
    arrived = lax.all_to_all(outgoing, ("dp", "expert"), 0, 0, tiled=True)
    produced = expert_block(
        arrived.reshape(devices * capacity, sub, lanes), gate_weight, up_weight, down_weight
    )
    returned = lax.all_to_all(
        produced.reshape(devices, capacity * sub, lanes), ("dp", "expert"), 0, 0, tiled=True
    )
    pieces = returned.reshape(experts, hidden_split, capacity, sub, lanes)[chosen, :, slots]
    blended = jnp.sum(pieces.astype(jnp.float32), axis=1) * expert_mix.reshape(-1)[:, None, None]
    expert_update = (
        jnp.sum(blended.reshape(tok_rows, TOP, sub, lanes), axis=1)
        .reshape(tok_rows, width)
        .astype(jnp.bfloat16)
    )
    return (attention_update, expert_update)


def solution(mesh):
    in_specs = (
        P(("dp", "expert"), None),
        P(),
        P(None, "expert"),
        P(None, "expert"),
        P(None, "expert"),
        P("expert", None),
        P("dp", None, "expert"),
        P("dp", None, "expert"),
        P("dp", None),
        P("dp"),
        P("dp"),
        P(),
        P(("dp", "expert"), None),
        P(("dp", "expert"), None),
        P(("dp", "expert"), None, None),
        P(("dp", "expert"), None, None),
        P(("dp", "expert"), None, None),
    )
    out_specs = (P(("dp", "expert"), None), P(("dp", "expert"), None))
    return jax.shard_map(
        per_device, mesh=mesh, in_specs=in_specs, out_specs=out_specs, check_vma=False
    )
```

```python
import jax
import jax.numpy as jnp
from jax import lax
from jax.sharding import PartitionSpec as P

HD = 128
FF = 1024
TOP = 8
GSIZE = 16
SB = 32


epsilon = 1e-06


def rms_scale(values, gain):
    widened = values.astype(jnp.float32)
    spread = jnp.mean(widened * widened, axis=-1, keepdims=True)
    return (widened * lax.rsqrt(spread + epsilon) * gain).astype(jnp.bfloat16)


def expert_block(block, gate_weight, up_weight, down_weight):
    rows, sub, lanes = block.shape
    gate = gate_weight[0].reshape(sub, lanes, -1)
    up = up_weight[0].reshape(sub, lanes, -1)
    contract = (((1, 2), (0, 1)), ((), ()))
    gated = lax.dot_general(block, gate, contract, preferred_element_type=jnp.float32)
    lifted = lax.dot_general(block, up, contract, preferred_element_type=jnp.float32)
    hidden = (jax.nn.silu(gated) * lifted).astype(jnp.bfloat16)
    produced = jnp.dot(hidden, down_weight[0], preferred_element_type=jnp.float32)
    return produced.astype(jnp.bfloat16).reshape(rows, sub, lanes)


def per_device(
    residual_in,
    attention_gain,
    query_weight,
    key_weight,
    value_weight,
    output_weight,
    prompt_keys,
    prompt_values,
    group_index,
    prompt_length,
    own_length,
    expert_gain,
    expert_ids,
    expert_mix,
    gate_weight,
    up_weight,
    down_weight,
):
    tok_rows, width = residual_in.shape
    local_width = query_weight.shape[1]
    heads_here = local_width // HD
    requests = group_index.shape[1]
    longest = prompt_keys.shape[1]
    groups_here = prompt_keys.shape[0]
    normed = rms_scale(residual_in, attention_gain)
    expert_groups = lax.axis_size("expert")
    copies = jnp.broadcast_to(normed[None], (expert_groups, tok_rows, width))
    piece = lax.all_to_all(copies, "expert", 0, 0, tiled=True).reshape(-1, width)
    query_part = jnp.dot(piece, query_weight, preferred_element_type=jnp.float32).astype(
        jnp.bfloat16
    )
    key_part = jnp.dot(piece, key_weight, preferred_element_type=jnp.float32).astype(jnp.bfloat16)
    value_part = jnp.dot(piece, value_weight, preferred_element_type=jnp.float32).astype(
        jnp.bfloat16
    )
    projected = jnp.concatenate([query_part, key_part, value_part], axis=1)
    layout = (requests, SB, heads_here, HD)
    queries = projected[:, :local_width].reshape(layout)
    new_keys = projected[:, local_width : 2 * local_width].reshape(layout)
    new_values = projected[:, 2 * local_width :].reshape(layout)
    scale = HD ** (-0.5)
    positions = jnp.arange(SB, dtype=jnp.int32)
    own_scores = (
        jnp.einsum("rihd,rjhd->rhij", queries, new_keys, preferred_element_type=jnp.float32) * scale
    )
    own_scores = jnp.where(
        positions[None, None, None, :] < own_length[:, None, None, None], own_scores, -jnp.inf
    )
    member = group_index[0]
    prompt_positions = jnp.arange(longest, dtype=jnp.int32)

    def group_step(group, attended):
        first = jnp.sum((member < group).astype(jnp.int32))
        start = jnp.minimum(first, requests - GSIZE)
        window_queries = lax.dynamic_slice_in_dim(queries, start, GSIZE, 0)
        group_keys = lax.dynamic_index_in_dim(prompt_keys, group, 0, keepdims=False).reshape(
            longest, heads_here, HD
        )
        group_values = lax.dynamic_index_in_dim(prompt_values, group, 0, keepdims=False).reshape(
            longest, heads_here, HD
        )
        scores = (
            jnp.einsum(
                "rihd,jhd->rhij", window_queries, group_keys, preferred_element_type=jnp.float32
            )
            * scale
        )
        limit = lax.dynamic_index_in_dim(prompt_length, group, 0, keepdims=False)
        scores = jnp.where(prompt_positions < limit, scores, -jnp.inf)
        window_own = lax.dynamic_slice_in_dim(own_scores, start, GSIZE, 0)
        highest = jnp.maximum(jnp.max(scores, axis=-1), jnp.max(window_own, axis=-1))
        prompt_weights = jnp.exp(scores - highest[..., None]).astype(jnp.bfloat16)
        own_weights = jnp.exp(window_own - highest[..., None]).astype(jnp.bfloat16)
        window_values = lax.dynamic_slice_in_dim(new_values, start, GSIZE, 0)
        summed = jnp.einsum(
            "rhij,jhd->rihd", prompt_weights, group_values, preferred_element_type=jnp.float32
        )
        summed = summed + jnp.einsum(
            "rhij,rjhd->rihd", own_weights, window_values, preferred_element_type=jnp.float32
        )
        totals = jnp.sum(prompt_weights, axis=-1, dtype=jnp.float32) + jnp.sum(
            own_weights, axis=-1, dtype=jnp.float32
        )
        result = (summed / jnp.transpose(totals, (0, 2, 1))[..., None]).astype(jnp.bfloat16)
        inside = lax.dynamic_slice_in_dim(member, start, GSIZE, 0) == group
        current = lax.dynamic_slice_in_dim(attended, start, GSIZE, 0)
        merged = jnp.where(inside[:, None, None, None], result, current)
        return lax.dynamic_update_slice_in_dim(attended, merged, start, 0)

    attended = lax.fori_loop(0, groups_here, group_step, jnp.zeros(layout, jnp.bfloat16))
    flat_attended = attended.reshape(requests * SB, local_width)
    piece = flat_attended
    projected_out = jnp.dot(piece, output_weight, preferred_element_type=jnp.float32).astype(jnp.bfloat16)
    partials = lax.all_to_all(
        projected_out.reshape(expert_groups, tok_rows, width), "expert", 0, 0, tiled=True
    )
    attention_update = jnp.sum(partials.astype(jnp.float32), axis=0).astype(jnp.bfloat16)
    expert_input = rms_scale(
        residual_in.astype(jnp.float32) + attention_update.astype(jnp.float32), expert_gain
    )
    data_groups = lax.axis_size("dp")
    devices = data_groups * expert_groups
    hidden_split = FF // gate_weight.shape[2]
    experts = devices // hidden_split
    capacity = max(2, tok_rows * TOP * 3 // (2 * experts))
    chosen = expert_ids.reshape(-1)
    routes_here = chosen.shape[0]
    owners = jnp.arange(routes_here, dtype=jnp.int32) // TOP
    matches = (chosen[:, None] == jnp.arange(experts, dtype=jnp.int32)[None, :]).astype(jnp.int32)
    slots = jnp.sum((jnp.cumsum(matches, axis=0) - matches) * matches, axis=1)
    table = (
        jnp.full((experts * capacity,), tok_rows, jnp.int32)
        .at[chosen * capacity + slots]
        .set(owners)
    )
    lanes = 128
    sub = width // lanes
    tiles = expert_input.reshape(tok_rows, sub, lanes)
    padded = jnp.concatenate([tiles, jnp.zeros((1, sub, lanes), jnp.bfloat16)], axis=0)
    index = jnp.broadcast_to(
        table.reshape(experts, 1, capacity), (experts, hidden_split, capacity)
    ).reshape(-1)
    outgoing = padded[index].reshape(devices, capacity * sub, lanes)
    arrived = lax.all_to_all(outgoing, ("dp", "expert"), 0, 0, tiled=True)
    produced = expert_block(
        arrived.reshape(devices * capacity, sub, lanes), gate_weight, up_weight, down_weight
    )
    returned = lax.all_to_all(
        produced.reshape(devices, capacity * sub, lanes), ("dp", "expert"), 0, 0, tiled=True
    )
    pieces = returned.reshape(experts, hidden_split, capacity, sub, lanes)[chosen, :, slots]
    blended = jnp.sum(pieces.astype(jnp.float32), axis=1) * expert_mix.reshape(-1)[:, None, None]
    expert_update = (
        jnp.sum(blended.reshape(tok_rows, TOP, sub, lanes), axis=1)
        .reshape(tok_rows, width)
        .astype(jnp.bfloat16)
    )
    return (attention_update, expert_update)


def solution(mesh):
    in_specs = (
        P(("dp", "expert"), None),
        P(),
        P(None, "expert"),
        P(None, "expert"),
        P(None, "expert"),
        P("expert", None),
        P("dp", None, "expert"),
        P("dp", None, "expert"),
        P("dp", None),
        P("dp"),
        P("dp"),
        P(),
        P(("dp", "expert"), None),
        P(("dp", "expert"), None),
        P(("dp", "expert"), None, None),
        P(("dp", "expert"), None, None),
        P(("dp", "expert"), None, None),
    )
    out_specs = (P(("dp", "expert"), None), P(("dp", "expert"), None))
    return jax.shard_map(
        per_device, mesh=mesh, in_specs=in_specs, out_specs=out_specs, check_vma=False
    )
```

```python
import math

import jax
import jax.numpy as jnp
from jax import lax
from jax.sharding import PartitionSpec as P

HD = 128
FF = 1024
TOP = 8
GSIZE = 16
SB = 32


epsilon = 1e-06


def rms_scale(values, gain):
    widened = values.astype(jnp.float32)
    spread = jnp.mean(widened * widened, axis=-1, keepdims=True)
    return (widened * lax.rsqrt(spread + epsilon) * gain).astype(jnp.bfloat16)


def expert_block(block, gate_weight, up_weight, down_weight):
    rows, sub, lanes = block.shape
    gate = gate_weight[0].reshape(sub, lanes, -1)
    up = up_weight[0].reshape(sub, lanes, -1)
    contract = (((1, 2), (0, 1)), ((), ()))
    gated = lax.dot_general(block, gate, contract, preferred_element_type=jnp.float32)
    lifted = lax.dot_general(block, up, contract, preferred_element_type=jnp.float32)
    hidden = (jax.nn.silu(gated) * lifted).astype(jnp.bfloat16)
    produced = jnp.dot(hidden, down_weight[0], preferred_element_type=jnp.float32)
    return produced.astype(jnp.bfloat16).reshape(rows, sub, lanes)


def ring_shift(block, side, along_x, step):
    pairs = []
    for source in range(side * side):
        row, column = divmod(source, side)
        if along_x:
            target = ((row + step) % side) * side + column
        else:
            target = row * side + (column + step) % side
        pairs.append((source, target))
    return lax.ppermute(block, "expert", pairs)


def ring_gather(block, side, along_x):
    assert side == 4
    from_left = ring_shift(block, side, along_x, 1)
    from_right = ring_shift(block, side, along_x, -1)
    cut = block.shape[-2] // 2
    far = jnp.concatenate(
        [
            ring_shift(from_left[..., :cut, :], side, along_x, 1),
            ring_shift(from_right[..., cut:, :], side, along_x, -1),
        ],
        axis=-2,
    )
    return jnp.stack([block, from_right, far, from_left])


def per_device(
    residual_in,
    attention_gain,
    query_weight,
    key_weight,
    value_weight,
    output_weight,
    prompt_keys,
    prompt_values,
    group_index,
    prompt_length,
    own_length,
    expert_gain,
    expert_ids,
    expert_mix,
    gate_weight,
    up_weight,
    down_weight,
):
    tok_rows, width = residual_in.shape
    local_width = query_weight.shape[1]
    heads_here = local_width // HD
    requests = group_index.shape[1]
    longest = prompt_keys.shape[1]
    groups_here = prompt_keys.shape[0]
    normed = rms_scale(residual_in, attention_gain)
    expert_groups = lax.axis_size("expert")
    side = math.isqrt(expert_groups)
    half = tok_rows // 2
    first = ring_gather(normed[:half], side, True)
    second = ring_gather(normed[half:], side, False)
    first = ring_gather(first, side, False)
    second = ring_gather(second, side, True)
    joined = jnp.concatenate([query_weight, key_weight, value_weight], axis=1)
    first = jnp.dot(first.reshape(-1, width), joined, preferred_element_type=jnp.float32)
    second = jnp.dot(second.reshape(-1, width), joined, preferred_element_type=jnp.float32)
    first = jnp.swapaxes(first.astype(jnp.bfloat16).reshape(side, side, half, -1), 0, 1)
    second = second.astype(jnp.bfloat16).reshape(side, side, half, -1)
    relative = jnp.concatenate([first, second], axis=2)
    place = lax.axis_index("expert")
    offsets = jnp.arange(side, dtype=jnp.int32)
    across = (offsets - place // side) % side
    down = (offsets - place % side) % side
    projected = relative[across][:, down].reshape(expert_groups * tok_rows, -1)
    layout = (requests, SB, heads_here, HD)
    queries = projected[:, :local_width].reshape(layout)
    new_keys = projected[:, local_width : 2 * local_width].reshape(layout)
    new_values = projected[:, 2 * local_width :].reshape(layout)
    scale = HD ** (-0.5)
    positions = jnp.arange(SB, dtype=jnp.int32)
    own_scores = (
        jnp.einsum("rihd,rjhd->rhij", queries, new_keys, preferred_element_type=jnp.float32) * scale
    )
    own_scores = jnp.where(
        positions[None, None, None, :] < own_length[:, None, None, None], own_scores, -jnp.inf
    )
    member = group_index[0]
    prompt_positions = jnp.arange(longest, dtype=jnp.int32)

    def group_step(group, attended):
        first = jnp.sum((member < group).astype(jnp.int32))
        start = jnp.minimum(first, requests - GSIZE)
        window_queries = lax.dynamic_slice_in_dim(queries, start, GSIZE, 0)
        group_keys = lax.dynamic_index_in_dim(prompt_keys, group, 0, keepdims=False).reshape(
            longest, heads_here, HD
        )
        group_values = lax.dynamic_index_in_dim(prompt_values, group, 0, keepdims=False).reshape(
            longest, heads_here, HD
        )
        scores = (
            jnp.einsum(
                "rihd,jhd->rhij", window_queries, group_keys, preferred_element_type=jnp.float32
            )
            * scale
        )
        limit = lax.dynamic_index_in_dim(prompt_length, group, 0, keepdims=False)
        scores = jnp.where(prompt_positions < limit, scores, -jnp.inf)
        window_own = lax.dynamic_slice_in_dim(own_scores, start, GSIZE, 0)
        highest = jnp.maximum(jnp.max(scores, axis=-1), jnp.max(window_own, axis=-1))
        prompt_weights = jnp.exp(scores - highest[..., None]).astype(jnp.bfloat16)
        own_weights = jnp.exp(window_own - highest[..., None]).astype(jnp.bfloat16)
        window_values = lax.dynamic_slice_in_dim(new_values, start, GSIZE, 0)
        summed = jnp.einsum(
            "rhij,jhd->rihd", prompt_weights, group_values, preferred_element_type=jnp.float32
        )
        summed = summed + jnp.einsum(
            "rhij,rjhd->rihd", own_weights, window_values, preferred_element_type=jnp.float32
        )
        totals = jnp.sum(prompt_weights, axis=-1, dtype=jnp.float32) + jnp.sum(
            own_weights, axis=-1, dtype=jnp.float32
        )
        result = (summed / jnp.transpose(totals, (0, 2, 1))[..., None]).astype(jnp.bfloat16)
        inside = lax.dynamic_slice_in_dim(member, start, GSIZE, 0) == group
        current = lax.dynamic_slice_in_dim(attended, start, GSIZE, 0)
        merged = jnp.where(inside[:, None, None, None], result, current)
        return lax.dynamic_update_slice_in_dim(attended, merged, start, 0)

    attended = lax.fori_loop(0, groups_here, group_step, jnp.zeros(layout, jnp.bfloat16))
    flat_attended = attended.reshape(requests * SB, local_width)
    piece = flat_attended
    projected_out = jnp.dot(piece, output_weight, preferred_element_type=jnp.float32).astype(jnp.bfloat16)
    partials = lax.all_to_all(
        projected_out.reshape(expert_groups, tok_rows, width), "expert", 0, 0, tiled=True
    )
    attention_update = jnp.sum(partials.astype(jnp.float32), axis=0).astype(jnp.bfloat16)
    expert_input = rms_scale(
        residual_in.astype(jnp.float32) + attention_update.astype(jnp.float32), expert_gain
    )
    data_groups = lax.axis_size("dp")
    devices = data_groups * expert_groups
    hidden_split = FF // gate_weight.shape[2]
    experts = devices // hidden_split
    capacity = max(2, tok_rows * TOP * 3 // (2 * experts))
    chosen = expert_ids.reshape(-1)
    routes_here = chosen.shape[0]
    owners = jnp.arange(routes_here, dtype=jnp.int32) // TOP
    matches = (chosen[:, None] == jnp.arange(experts, dtype=jnp.int32)[None, :]).astype(jnp.int32)
    slots = jnp.sum((jnp.cumsum(matches, axis=0) - matches) * matches, axis=1)
    table = (
        jnp.full((experts * capacity,), tok_rows, jnp.int32)
        .at[chosen * capacity + slots]
        .set(owners)
    )
    lanes = 128
    sub = width // lanes
    tiles = expert_input.reshape(tok_rows, sub, lanes)
    padded = jnp.concatenate([tiles, jnp.zeros((1, sub, lanes), jnp.bfloat16)], axis=0)
    index = jnp.broadcast_to(
        table.reshape(experts, 1, capacity), (experts, hidden_split, capacity)
    ).reshape(-1)
    outgoing = padded[index].reshape(devices, capacity * sub, lanes)
    arrived = lax.all_to_all(outgoing, ("dp", "expert"), 0, 0, tiled=True)
    produced = expert_block(
        arrived.reshape(devices * capacity, sub, lanes), gate_weight, up_weight, down_weight
    )
    returned = lax.all_to_all(
        produced.reshape(devices, capacity * sub, lanes), ("dp", "expert"), 0, 0, tiled=True
    )
    pieces = returned.reshape(experts, hidden_split, capacity, sub, lanes)[chosen, :, slots]
    blended = jnp.sum(pieces.astype(jnp.float32), axis=1) * expert_mix.reshape(-1)[:, None, None]
    expert_update = (
        jnp.sum(blended.reshape(tok_rows, TOP, sub, lanes), axis=1)
        .reshape(tok_rows, width)
        .astype(jnp.bfloat16)
    )
    return (attention_update, expert_update)


def solution(mesh):
    in_specs = (
        P(("dp", "expert"), None),
        P(),
        P(None, "expert"),
        P(None, "expert"),
        P(None, "expert"),
        P("expert", None),
        P("dp", None, "expert"),
        P("dp", None, "expert"),
        P("dp", None),
        P("dp"),
        P("dp"),
        P(),
        P(("dp", "expert"), None),
        P(("dp", "expert"), None),
        P(("dp", "expert"), None, None),
        P(("dp", "expert"), None, None),
        P(("dp", "expert"), None, None),
    )
    out_specs = (P(("dp", "expert"), None), P(("dp", "expert"), None))
    return jax.shard_map(
        per_device, mesh=mesh, in_specs=in_specs, out_specs=out_specs, check_vma=False
    )
```

```python
import math

import jax
import jax.numpy as jnp
from jax import lax
from jax.sharding import PartitionSpec as P

HD = 128
FF = 1024
TOP = 8
GSIZE = 16
SB = 32


epsilon = 1e-06


def rms_scale(values, gain):
    widened = values.astype(jnp.float32)
    spread = jnp.mean(widened * widened, axis=-1, keepdims=True)
    return (widened * lax.rsqrt(spread + epsilon) * gain).astype(jnp.bfloat16)


def expert_block(block, gate_weight, up_weight, down_weight):
    rows, sub, lanes = block.shape
    gate = gate_weight[0].reshape(sub, lanes, -1)
    up = up_weight[0].reshape(sub, lanes, -1)
    contract = (((1, 2), (0, 1)), ((), ()))
    gated = lax.dot_general(block, gate, contract, preferred_element_type=jnp.float32)
    lifted = lax.dot_general(block, up, contract, preferred_element_type=jnp.float32)
    hidden = (jax.nn.silu(gated) * lifted).astype(jnp.bfloat16)
    produced = jnp.dot(hidden, down_weight[0], preferred_element_type=jnp.float32)
    return produced.astype(jnp.bfloat16).reshape(rows, sub, lanes)


def ring_shift(block, side, along_x, step):
    pairs = []
    for source in range(side * side):
        row, column = divmod(source, side)
        if along_x:
            target = ((row + step) % side) * side + column
        else:
            target = row * side + (column + step) % side
        pairs.append((source, target))
    return lax.ppermute(block, "expert", pairs)


def ring_gather(block, side, along_x):
    assert side == 4
    from_left = ring_shift(block, side, along_x, 1)
    from_right = ring_shift(block, side, along_x, -1)
    cut = block.shape[-2] // 2
    far = jnp.concatenate(
        [
            ring_shift(from_left[..., :cut, :], side, along_x, 1),
            ring_shift(from_right[..., cut:, :], side, along_x, -1),
        ],
        axis=-2,
    )
    return jnp.stack([block, from_right, far, from_left])


def ring_reduce(relative, side, along_x):
    assert side == 4
    cut = relative.shape[-2] // 2
    far = relative[2].astype(jnp.bfloat16)
    came_left = ring_shift(far[..., :cut, :], side, along_x, 1).astype(jnp.float32)
    came_right = ring_shift(far[..., cut:, :], side, along_x, -1).astype(jnp.float32)
    rightward = jnp.concatenate([relative[1][..., :cut, :] + came_left, relative[1][..., cut:, :]], axis=-2)
    leftward = jnp.concatenate([relative[3][..., :cut, :], relative[3][..., cut:, :] + came_right], axis=-2)
    from_left = ring_shift(rightward.astype(jnp.bfloat16), side, along_x, 1)
    from_right = ring_shift(leftward.astype(jnp.bfloat16), side, along_x, -1)
    return relative[0] + from_left.astype(jnp.float32) + from_right.astype(jnp.float32)


def per_device(
    residual_in,
    attention_gain,
    query_weight,
    key_weight,
    value_weight,
    output_weight,
    prompt_keys,
    prompt_values,
    group_index,
    prompt_length,
    own_length,
    expert_gain,
    expert_ids,
    expert_mix,
    gate_weight,
    up_weight,
    down_weight,
):
    tok_rows, width = residual_in.shape
    local_width = query_weight.shape[1]
    heads_here = local_width // HD
    requests = group_index.shape[1]
    longest = prompt_keys.shape[1]
    groups_here = prompt_keys.shape[0]
    normed = rms_scale(residual_in, attention_gain)
    expert_groups = lax.axis_size("expert")
    side = math.isqrt(expert_groups)
    half = tok_rows // 2
    first = ring_gather(normed[:half], side, True)
    second = ring_gather(normed[half:], side, False)
    first = ring_gather(first, side, False)
    second = ring_gather(second, side, True)
    joined = jnp.concatenate([query_weight, key_weight, value_weight], axis=1)
    first = jnp.dot(first.reshape(-1, width), joined, preferred_element_type=jnp.float32)
    second = jnp.dot(second.reshape(-1, width), joined, preferred_element_type=jnp.float32)
    first = jnp.swapaxes(first.astype(jnp.bfloat16).reshape(side, side, half, -1), 0, 1)
    second = second.astype(jnp.bfloat16).reshape(side, side, half, -1)
    relative = jnp.concatenate([first, second], axis=2)
    place = lax.axis_index("expert")
    offsets = jnp.arange(side, dtype=jnp.int32)
    across = (offsets - place // side) % side
    down = (offsets - place % side) % side
    projected = relative[across][:, down].reshape(expert_groups * tok_rows, -1)
    layout = (requests, SB, heads_here, HD)
    queries = projected[:, :local_width].reshape(layout)
    new_keys = projected[:, local_width : 2 * local_width].reshape(layout)
    new_values = projected[:, 2 * local_width :].reshape(layout)
    scale = HD ** (-0.5)
    positions = jnp.arange(SB, dtype=jnp.int32)
    own_scores = (
        jnp.einsum("rihd,rjhd->rhij", queries, new_keys, preferred_element_type=jnp.float32) * scale
    )
    own_scores = jnp.where(
        positions[None, None, None, :] < own_length[:, None, None, None], own_scores, -jnp.inf
    )
    member = group_index[0]
    prompt_positions = jnp.arange(longest, dtype=jnp.int32)

    def group_step(group, attended):
        first = jnp.sum((member < group).astype(jnp.int32))
        start = jnp.minimum(first, requests - GSIZE)
        window_queries = lax.dynamic_slice_in_dim(queries, start, GSIZE, 0)
        group_keys = lax.dynamic_index_in_dim(prompt_keys, group, 0, keepdims=False).reshape(
            longest, heads_here, HD
        )
        group_values = lax.dynamic_index_in_dim(prompt_values, group, 0, keepdims=False).reshape(
            longest, heads_here, HD
        )
        scores = (
            jnp.einsum(
                "rihd,jhd->rhij", window_queries, group_keys, preferred_element_type=jnp.float32
            )
            * scale
        )
        limit = lax.dynamic_index_in_dim(prompt_length, group, 0, keepdims=False)
        scores = jnp.where(prompt_positions < limit, scores, -jnp.inf)
        window_own = lax.dynamic_slice_in_dim(own_scores, start, GSIZE, 0)
        highest = jnp.maximum(jnp.max(scores, axis=-1), jnp.max(window_own, axis=-1))
        prompt_weights = jnp.exp(scores - highest[..., None]).astype(jnp.bfloat16)
        own_weights = jnp.exp(window_own - highest[..., None]).astype(jnp.bfloat16)
        window_values = lax.dynamic_slice_in_dim(new_values, start, GSIZE, 0)
        summed = jnp.einsum(
            "rhij,jhd->rihd", prompt_weights, group_values, preferred_element_type=jnp.float32
        )
        summed = summed + jnp.einsum(
            "rhij,rjhd->rihd", own_weights, window_values, preferred_element_type=jnp.float32
        )
        totals = jnp.sum(prompt_weights, axis=-1, dtype=jnp.float32) + jnp.sum(
            own_weights, axis=-1, dtype=jnp.float32
        )
        result = (summed / jnp.transpose(totals, (0, 2, 1))[..., None]).astype(jnp.bfloat16)
        inside = lax.dynamic_slice_in_dim(member, start, GSIZE, 0) == group
        current = lax.dynamic_slice_in_dim(attended, start, GSIZE, 0)
        merged = jnp.where(inside[:, None, None, None], result, current)
        return lax.dynamic_update_slice_in_dim(attended, merged, start, 0)

    attended = lax.fori_loop(0, groups_here, group_step, jnp.zeros(layout, jnp.bfloat16))
    owners = attended.reshape(side, side, tok_rows, local_width)
    ahead_x = (offsets + place // side) % side
    ahead_y = (offsets + place % side) % side
    owners = owners[ahead_x][:, ahead_y]
    first = owners[:, :, :half].reshape(-1, local_width)
    second = jnp.swapaxes(owners[:, :, half:], 0, 1).reshape(-1, local_width)
    first = jnp.dot(first, output_weight, preferred_element_type=jnp.float32)
    second = jnp.dot(second, output_weight, preferred_element_type=jnp.float32)
    first = ring_reduce(first.reshape(side, side, half, width), side, True)
    second = ring_reduce(second.reshape(side, side, half, width), side, False)
    first = ring_reduce(first, side, False)
    second = ring_reduce(second, side, True)
    attention_update = jnp.concatenate([first, second], axis=0).astype(jnp.bfloat16)
    expert_input = rms_scale(
        residual_in.astype(jnp.float32) + attention_update.astype(jnp.float32), expert_gain
    )
    data_groups = lax.axis_size("dp")
    devices = data_groups * expert_groups
    hidden_split = FF // gate_weight.shape[2]
    experts = devices // hidden_split
    capacity = max(2, tok_rows * TOP * 3 // (2 * experts))
    chosen = expert_ids.reshape(-1)
    routes_here = chosen.shape[0]
    owners = jnp.arange(routes_here, dtype=jnp.int32) // TOP
    matches = (chosen[:, None] == jnp.arange(experts, dtype=jnp.int32)[None, :]).astype(jnp.int32)
    slots = jnp.sum((jnp.cumsum(matches, axis=0) - matches) * matches, axis=1)
    table = (
        jnp.full((experts * capacity,), tok_rows, jnp.int32)
        .at[chosen * capacity + slots]
        .set(owners)
    )
    lanes = 128
    sub = width // lanes
    tiles = expert_input.reshape(tok_rows, sub, lanes)
    padded = jnp.concatenate([tiles, jnp.zeros((1, sub, lanes), jnp.bfloat16)], axis=0)
    index = jnp.broadcast_to(
        table.reshape(experts, 1, capacity), (experts, hidden_split, capacity)
    ).reshape(-1)
    outgoing = padded[index].reshape(devices, capacity * sub, lanes)
    arrived = lax.all_to_all(outgoing, ("dp", "expert"), 0, 0, tiled=True)
    produced = expert_block(
        arrived.reshape(devices * capacity, sub, lanes), gate_weight, up_weight, down_weight
    )
    returned = lax.all_to_all(
        produced.reshape(devices, capacity * sub, lanes), ("dp", "expert"), 0, 0, tiled=True
    )
    pieces = returned.reshape(experts, hidden_split, capacity, sub, lanes)[chosen, :, slots]
    blended = jnp.sum(pieces.astype(jnp.float32), axis=1) * expert_mix.reshape(-1)[:, None, None]
    expert_update = (
        jnp.sum(blended.reshape(tok_rows, TOP, sub, lanes), axis=1)
        .reshape(tok_rows, width)
        .astype(jnp.bfloat16)
    )
    return (attention_update, expert_update)


def solution(mesh):
    in_specs = (
        P(("dp", "expert"), None),
        P(),
        P(None, "expert"),
        P(None, "expert"),
        P(None, "expert"),
        P("expert", None),
        P("dp", None, "expert"),
        P("dp", None, "expert"),
        P("dp", None),
        P("dp"),
        P("dp"),
        P(),
        P(("dp", "expert"), None),
        P(("dp", "expert"), None),
        P(("dp", "expert"), None, None),
        P(("dp", "expert"), None, None),
        P(("dp", "expert"), None, None),
    )
    out_specs = (P(("dp", "expert"), None), P(("dp", "expert"), None))
    return jax.shard_map(
        per_device, mesh=mesh, in_specs=in_specs, out_specs=out_specs, check_vma=False
    )
```

```python
import math

import jax
import jax.numpy as jnp
from jax import lax
from jax.experimental import pallas as pl
from jax.experimental.pallas import tpu as pltpu
from jax.sharding import PartitionSpec as P

HD = 128
FF = 1024
TOP = 8
GSIZE = 16
SB = 32


epsilon = 1e-06


def rms_scale(values, gain):
    widened = values.astype(jnp.float32)
    spread = jnp.mean(widened * widened, axis=-1, keepdims=True)
    return (widened * lax.rsqrt(spread + epsilon) * gain).astype(jnp.bfloat16)


def expert_block(block, gate_weight, up_weight, down_weight):
    rows, sub, lanes = block.shape
    gate = gate_weight[0].reshape(sub, lanes, -1)
    up = up_weight[0].reshape(sub, lanes, -1)
    contract = (((1, 2), (0, 1)), ((), ()))
    gated = lax.dot_general(block, gate, contract, preferred_element_type=jnp.float32)
    lifted = lax.dot_general(block, up, contract, preferred_element_type=jnp.float32)
    hidden = (jax.nn.silu(gated) * lifted).astype(jnp.bfloat16)
    produced = jnp.dot(hidden, down_weight[0], preferred_element_type=jnp.float32)
    return produced.astype(jnp.bfloat16).reshape(rows, sub, lanes)


def attend_kernel(limit_ref, q_ref, k_ref, v_ref, ok_ref, ov_ref, om_ref, o_ref):
    scale = HD ** (-0.5)
    q = q_ref[...]
    batch, block, depth = q.shape
    rows = batch * block
    scores = lax.dot_general(
        q.reshape(rows, depth), k_ref[...], (((1,), (1,)), ((), ())),
        preferred_element_type=jnp.float32) * scale
    column = lax.broadcasted_iota(jnp.int32, scores.shape, 1)
    scores = jnp.where(column < limit_ref[0], scores, -jnp.inf)
    own = jnp.einsum("rid,rjd->rij", q, ok_ref[...], preferred_element_type=jnp.float32) * scale
    own = own + om_ref[...]
    highest = jnp.maximum(
        jnp.max(scores, axis=1, keepdims=True),
        jnp.max(own, axis=2, keepdims=True).reshape(rows, 1))
    weights = jnp.exp(scores - highest).astype(jnp.bfloat16)
    own_weights = jnp.exp(own - highest.reshape(batch, block, 1)).astype(jnp.bfloat16)
    summed = jnp.dot(weights, v_ref[...], preferred_element_type=jnp.float32)
    summed = summed.reshape(batch, block, depth) + jnp.einsum(
        "rij,rjd->rid", own_weights, ov_ref[...], preferred_element_type=jnp.float32)
    totals = jnp.sum(weights.astype(jnp.float32), axis=1, keepdims=True).reshape(batch, block, 1)
    totals = totals + jnp.sum(own_weights.astype(jnp.float32), axis=2, keepdims=True)
    o_ref[...] = (summed / totals).astype(o_ref.dtype)


def attend_window(limit, q, k, v, ok, ov, om):
    vmem = pl.BlockSpec(memory_space=pltpu.VMEM)
    return pl.pallas_call(
        attend_kernel,
        out_shape=jax.ShapeDtypeStruct(q.shape, jnp.bfloat16),
        in_specs=[pl.BlockSpec(memory_space=pltpu.SMEM)] + [vmem] * 6,
        out_specs=vmem,
    )(limit, q, k, v, ok, ov, om)


def ring_shift(block, side, along_x, step):
    pairs = []
    for source in range(side * side):
        row, column = divmod(source, side)
        if along_x:
            target = ((row + step) % side) * side + column
        else:
            target = row * side + (column + step) % side
        pairs.append((source, target))
    return lax.ppermute(block, "expert", pairs)


def ring_gather(block, side, along_x):
    assert side == 4
    from_left = ring_shift(block, side, along_x, 1)
    from_right = ring_shift(block, side, along_x, -1)
    cut = block.shape[-2] // 2
    far = jnp.concatenate(
        [
            ring_shift(from_left[..., :cut, :], side, along_x, 1),
            ring_shift(from_right[..., cut:, :], side, along_x, -1),
        ],
        axis=-2,
    )
    return jnp.stack([block, from_right, far, from_left])


def ring_reduce(relative, side, along_x):
    assert side == 4
    cut = relative.shape[-2] // 2
    far = relative[2].astype(jnp.bfloat16)
    came_left = ring_shift(far[..., :cut, :], side, along_x, 1).astype(jnp.float32)
    came_right = ring_shift(far[..., cut:, :], side, along_x, -1).astype(jnp.float32)
    rightward = jnp.concatenate([relative[1][..., :cut, :] + came_left, relative[1][..., cut:, :]], axis=-2)
    leftward = jnp.concatenate([relative[3][..., :cut, :], relative[3][..., cut:, :] + came_right], axis=-2)
    from_left = ring_shift(rightward.astype(jnp.bfloat16), side, along_x, 1)
    from_right = ring_shift(leftward.astype(jnp.bfloat16), side, along_x, -1)
    return relative[0] + from_left.astype(jnp.float32) + from_right.astype(jnp.float32)


def per_device(
    residual_in,
    attention_gain,
    query_weight,
    key_weight,
    value_weight,
    output_weight,
    prompt_keys,
    prompt_values,
    group_index,
    prompt_length,
    own_length,
    expert_gain,
    expert_ids,
    expert_mix,
    gate_weight,
    up_weight,
    down_weight,
):
    tok_rows, width = residual_in.shape
    local_width = query_weight.shape[1]
    heads_here = local_width // HD
    requests = group_index.shape[1]
    longest = prompt_keys.shape[1]
    groups_here = prompt_keys.shape[0]
    normed = rms_scale(residual_in, attention_gain)
    expert_groups = lax.axis_size("expert")
    side = math.isqrt(expert_groups)
    half = tok_rows // 2
    first = ring_gather(normed[:half], side, True)
    second = ring_gather(normed[half:], side, False)
    first = ring_gather(first, side, False)
    second = ring_gather(second, side, True)
    joined = jnp.concatenate([query_weight, key_weight, value_weight], axis=1)
    first = jnp.dot(first.reshape(-1, width), joined, preferred_element_type=jnp.float32)
    second = jnp.dot(second.reshape(-1, width), joined, preferred_element_type=jnp.float32)
    first = jnp.swapaxes(first.astype(jnp.bfloat16).reshape(side, side, half, -1), 0, 1)
    second = second.astype(jnp.bfloat16).reshape(side, side, half, -1)
    relative = jnp.concatenate([first, second], axis=2)
    place = lax.axis_index("expert")
    offsets = jnp.arange(side, dtype=jnp.int32)
    across = (offsets - place // side) % side
    down = (offsets - place % side) % side
    projected = relative[across][:, down].reshape(expert_groups * tok_rows, -1)
    layout = (requests, SB, heads_here, HD)
    queries = projected[:, :local_width].reshape(layout)
    new_keys = projected[:, local_width : 2 * local_width].reshape(layout)
    new_values = projected[:, 2 * local_width :].reshape(layout)
    scale = HD ** (-0.5)
    positions = jnp.arange(SB, dtype=jnp.int32)
    assert heads_here == 1
    queries = queries.reshape(requests, SB, HD)
    new_keys = new_keys.reshape(requests, SB, HD)
    new_values = new_values.reshape(requests, SB, HD)
    own_mask = jnp.where(positions[None, :] < own_length[:, None], 0.0, -jnp.inf)
    own_mask = jnp.broadcast_to(own_mask[:, None, :], (requests, SB, SB)).astype(jnp.float32)
    member = group_index[0]

    def group_step(group, attended):
        first = jnp.sum((member < group).astype(jnp.int32))
        start = jnp.minimum(first, requests - GSIZE)
        window = lambda values: lax.dynamic_slice_in_dim(values, start, GSIZE, 0)
        group_keys = lax.dynamic_index_in_dim(prompt_keys, group, 0, keepdims=False)
        group_values = lax.dynamic_index_in_dim(prompt_values, group, 0, keepdims=False)
        limit = lax.dynamic_slice_in_dim(prompt_length, group, 1, 0)
        result = attend_window(
            limit,
            window(queries),
            group_keys,
            group_values,
            window(new_keys),
            window(new_values),
            window(own_mask),
        )
        inside = window(member) == group
        merged = jnp.where(inside[:, None, None], result, window(attended))
        return lax.dynamic_update_slice_in_dim(attended, merged, start, 0)

    attended = lax.fori_loop(
        0, groups_here, group_step, jnp.zeros((requests, SB, HD), jnp.bfloat16)
    )
    owners = attended.reshape(side, side, tok_rows, local_width)
    ahead_x = (offsets + place // side) % side
    ahead_y = (offsets + place % side) % side
    owners = owners[ahead_x][:, ahead_y]
    first = owners[:, :, :half].reshape(-1, local_width)
    second = jnp.swapaxes(owners[:, :, half:], 0, 1).reshape(-1, local_width)
    first = jnp.dot(first, output_weight, preferred_element_type=jnp.float32)
    second = jnp.dot(second, output_weight, preferred_element_type=jnp.float32)
    first = ring_reduce(first.reshape(side, side, half, width), side, True)
    second = ring_reduce(second.reshape(side, side, half, width), side, False)
    first = ring_reduce(first, side, False)
    second = ring_reduce(second, side, True)
    attention_update = jnp.concatenate([first, second], axis=0).astype(jnp.bfloat16)
    expert_input = rms_scale(
        residual_in.astype(jnp.float32) + attention_update.astype(jnp.float32), expert_gain
    )
    data_groups = lax.axis_size("dp")
    devices = data_groups * expert_groups
    hidden_split = FF // gate_weight.shape[2]
    experts = devices // hidden_split
    capacity = max(2, tok_rows * TOP * 3 // (2 * experts))
    chosen = expert_ids.reshape(-1)
    routes_here = chosen.shape[0]
    owners = jnp.arange(routes_here, dtype=jnp.int32) // TOP
    matches = (chosen[:, None] == jnp.arange(experts, dtype=jnp.int32)[None, :]).astype(jnp.int32)
    slots = jnp.sum((jnp.cumsum(matches, axis=0) - matches) * matches, axis=1)
    table = (
        jnp.full((experts * capacity,), tok_rows, jnp.int32)
        .at[chosen * capacity + slots]
        .set(owners)
    )
    lanes = 128
    sub = width // lanes
    tiles = expert_input.reshape(tok_rows, sub, lanes)
    padded = jnp.concatenate([tiles, jnp.zeros((1, sub, lanes), jnp.bfloat16)], axis=0)
    index = jnp.broadcast_to(
        table.reshape(experts, 1, capacity), (experts, hidden_split, capacity)
    ).reshape(-1)
    outgoing = padded[index].reshape(devices, capacity * sub, lanes)
    arrived = lax.all_to_all(outgoing, ("dp", "expert"), 0, 0, tiled=True)
    produced = expert_block(
        arrived.reshape(devices * capacity, sub, lanes), gate_weight, up_weight, down_weight
    )
    returned = lax.all_to_all(
        produced.reshape(devices, capacity * sub, lanes), ("dp", "expert"), 0, 0, tiled=True
    )
    pieces = returned.reshape(experts, hidden_split, capacity, sub, lanes)[chosen, :, slots]
    blended = jnp.sum(pieces.astype(jnp.float32), axis=1) * expert_mix.reshape(-1)[:, None, None]
    expert_update = (
        jnp.sum(blended.reshape(tok_rows, TOP, sub, lanes), axis=1)
        .reshape(tok_rows, width)
        .astype(jnp.bfloat16)
    )
    return (attention_update, expert_update)


def solution(mesh):
    in_specs = (
        P(("dp", "expert"), None),
        P(),
        P(None, "expert"),
        P(None, "expert"),
        P(None, "expert"),
        P("expert", None),
        P("dp", None, "expert"),
        P("dp", None, "expert"),
        P("dp", None),
        P("dp"),
        P("dp"),
        P(),
        P(("dp", "expert"), None),
        P(("dp", "expert"), None),
        P(("dp", "expert"), None, None),
        P(("dp", "expert"), None, None),
        P(("dp", "expert"), None, None),
    )
    out_specs = (P(("dp", "expert"), None), P(("dp", "expert"), None))
    return jax.shard_map(
        per_device, mesh=mesh, in_specs=in_specs, out_specs=out_specs, check_vma=False
    )
```

```python
import math

import jax
import jax.numpy as jnp
from jax import lax
from jax.sharding import PartitionSpec as P

HD = 128
FF = 1024
TOP = 8
GSIZE = 16
SB = 32


epsilon = 1e-06


def rms_scale(values, gain):
    widened = values.astype(jnp.float32)
    spread = jnp.mean(widened * widened, axis=-1, keepdims=True)
    return (widened * lax.rsqrt(spread + epsilon) * gain).astype(jnp.bfloat16)


def expert_block(block, gate_weight, up_weight, down_weight):
    rows, sub, lanes = block.shape
    gate = gate_weight[0].reshape(sub, lanes, -1)
    up = up_weight[0].reshape(sub, lanes, -1)
    contract = (((1, 2), (0, 1)), ((), ()))
    gated = lax.dot_general(block, gate, contract, preferred_element_type=jnp.float32)
    lifted = lax.dot_general(block, up, contract, preferred_element_type=jnp.float32)
    hidden = (jax.nn.silu(gated) * lifted).astype(jnp.bfloat16)
    produced = jnp.dot(hidden, down_weight[0], preferred_element_type=jnp.float32)
    return produced.astype(jnp.bfloat16).reshape(rows, sub, lanes)


def ring_shift(block, side, along_x, step):
    pairs = []
    for source in range(side * side):
        row, column = divmod(source, side)
        if along_x:
            target = ((row + step) % side) * side + column
        else:
            target = row * side + (column + step) % side
        pairs.append((source, target))
    return lax.ppermute(block, "expert", pairs)


def ring_gather(block, side, along_x):
    assert side == 4
    from_left = ring_shift(block, side, along_x, 1)
    from_right = ring_shift(block, side, along_x, -1)
    cut = block.shape[-2] // 2
    far = jnp.concatenate(
        [
            ring_shift(block[..., :cut, :], side, along_x, 2),
            ring_shift(block[..., cut:, :], side, along_x, -2),
        ],
        axis=-2,
    )
    return jnp.stack([block, from_right, far, from_left])


def ring_reduce(relative, side, along_x):
    assert side == 4
    cut = relative.shape[-2] // 2
    narrow = relative.astype(jnp.bfloat16)
    from_left = ring_shift(narrow[1], side, along_x, 1).astype(jnp.float32)
    from_right = ring_shift(narrow[3], side, along_x, -1).astype(jnp.float32)
    far = jnp.concatenate(
        [
            ring_shift(narrow[2][..., :cut, :], side, along_x, 2),
            ring_shift(narrow[2][..., cut:, :], side, along_x, -2),
        ],
        axis=-2,
    ).astype(jnp.float32)
    return relative[0] + from_left + from_right + far


def per_device(
    residual_in,
    attention_gain,
    query_weight,
    key_weight,
    value_weight,
    output_weight,
    prompt_keys,
    prompt_values,
    group_index,
    prompt_length,
    own_length,
    expert_gain,
    expert_ids,
    expert_mix,
    gate_weight,
    up_weight,
    down_weight,
):
    tok_rows, width = residual_in.shape
    local_width = query_weight.shape[1]
    heads_here = local_width // HD
    requests = group_index.shape[1]
    longest = prompt_keys.shape[1]
    groups_here = prompt_keys.shape[0]
    normed = rms_scale(residual_in, attention_gain)
    expert_groups = lax.axis_size("expert")
    side = math.isqrt(expert_groups)
    half = tok_rows // 2
    first = ring_gather(normed[:half], side, True)
    second = ring_gather(normed[half:], side, False)
    first = ring_gather(first, side, False)
    second = ring_gather(second, side, True)
    joined = jnp.concatenate([query_weight, key_weight, value_weight], axis=1)
    first = jnp.dot(first.reshape(-1, width), joined, preferred_element_type=jnp.float32)
    second = jnp.dot(second.reshape(-1, width), joined, preferred_element_type=jnp.float32)
    first = jnp.swapaxes(first.astype(jnp.bfloat16).reshape(side, side, half, -1), 0, 1)
    second = second.astype(jnp.bfloat16).reshape(side, side, half, -1)
    relative = jnp.concatenate([first, second], axis=2)
    place = lax.axis_index("expert")
    offsets = jnp.arange(side, dtype=jnp.int32)
    across = (offsets - place // side) % side
    down = (offsets - place % side) % side
    projected = relative[across][:, down].reshape(expert_groups * tok_rows, -1)
    layout = (requests, SB, heads_here, HD)
    queries = projected[:, :local_width].reshape(layout)
    new_keys = projected[:, local_width : 2 * local_width].reshape(layout)
    new_values = projected[:, 2 * local_width :].reshape(layout)
    scale = HD ** (-0.5)
    positions = jnp.arange(SB, dtype=jnp.int32)
    own_scores = (
        jnp.einsum("rihd,rjhd->rhij", queries, new_keys, preferred_element_type=jnp.float32) * scale
    )
    own_scores = jnp.where(
        positions[None, None, None, :] < own_length[:, None, None, None], own_scores, -jnp.inf
    )
    member = group_index[0]
    prompt_positions = jnp.arange(longest, dtype=jnp.int32)

    def group_step(group, attended):
        first = jnp.sum((member < group).astype(jnp.int32))
        start = jnp.minimum(first, requests - GSIZE)
        window_queries = lax.dynamic_slice_in_dim(queries, start, GSIZE, 0)
        group_keys = lax.dynamic_index_in_dim(prompt_keys, group, 0, keepdims=False).reshape(
            longest, heads_here, HD
        )
        group_values = lax.dynamic_index_in_dim(prompt_values, group, 0, keepdims=False).reshape(
            longest, heads_here, HD
        )
        scores = (
            jnp.einsum(
                "rihd,jhd->rhij", window_queries, group_keys, preferred_element_type=jnp.float32
            )
            * scale
        )
        limit = lax.dynamic_index_in_dim(prompt_length, group, 0, keepdims=False)
        scores = jnp.where(prompt_positions < limit, scores, -jnp.inf)
        window_own = lax.dynamic_slice_in_dim(own_scores, start, GSIZE, 0)
        highest = jnp.maximum(jnp.max(scores, axis=-1), jnp.max(window_own, axis=-1))
        prompt_weights = jnp.exp(scores - highest[..., None]).astype(jnp.bfloat16)
        own_weights = jnp.exp(window_own - highest[..., None]).astype(jnp.bfloat16)
        window_values = lax.dynamic_slice_in_dim(new_values, start, GSIZE, 0)
        summed = jnp.einsum(
            "rhij,jhd->rihd", prompt_weights, group_values, preferred_element_type=jnp.float32
        )
        summed = summed + jnp.einsum(
            "rhij,rjhd->rihd", own_weights, window_values, preferred_element_type=jnp.float32
        )
        totals = jnp.sum(prompt_weights, axis=-1, dtype=jnp.float32) + jnp.sum(
            own_weights, axis=-1, dtype=jnp.float32
        )
        result = (summed / jnp.transpose(totals, (0, 2, 1))[..., None]).astype(jnp.bfloat16)
        inside = lax.dynamic_slice_in_dim(member, start, GSIZE, 0) == group
        current = lax.dynamic_slice_in_dim(attended, start, GSIZE, 0)
        merged = jnp.where(inside[:, None, None, None], result, current)
        return lax.dynamic_update_slice_in_dim(attended, merged, start, 0)

    attended = lax.fori_loop(0, groups_here, group_step, jnp.zeros(layout, jnp.bfloat16))
    owners = attended.reshape(side, side, tok_rows, local_width)
    ahead_x = (offsets + place // side) % side
    ahead_y = (offsets + place % side) % side
    owners = owners[ahead_x][:, ahead_y]
    first = owners[:, :, :half].reshape(-1, local_width)
    second = jnp.swapaxes(owners[:, :, half:], 0, 1).reshape(-1, local_width)
    first = jnp.dot(first, output_weight, preferred_element_type=jnp.float32)
    second = jnp.dot(second, output_weight, preferred_element_type=jnp.float32)
    first = ring_reduce(first.reshape(side, side, half, width), side, True)
    second = ring_reduce(second.reshape(side, side, half, width), side, False)
    first = ring_reduce(first, side, False)
    second = ring_reduce(second, side, True)
    attention_update = jnp.concatenate([first, second], axis=0).astype(jnp.bfloat16)
    expert_input = rms_scale(
        residual_in.astype(jnp.float32) + attention_update.astype(jnp.float32), expert_gain
    )
    data_groups = lax.axis_size("dp")
    devices = data_groups * expert_groups
    hidden_split = FF // gate_weight.shape[2]
    experts = devices // hidden_split
    capacity = max(2, tok_rows * TOP * 3 // (2 * experts))
    chosen = expert_ids.reshape(-1)
    routes_here = chosen.shape[0]
    owners = jnp.arange(routes_here, dtype=jnp.int32) // TOP
    matches = (chosen[:, None] == jnp.arange(experts, dtype=jnp.int32)[None, :]).astype(jnp.int32)
    slots = jnp.sum((jnp.cumsum(matches, axis=0) - matches) * matches, axis=1)
    table = (
        jnp.full((experts * capacity,), tok_rows, jnp.int32)
        .at[chosen * capacity + slots]
        .set(owners)
    )
    lanes = 128
    sub = width // lanes
    tiles = expert_input.reshape(tok_rows, sub, lanes)
    padded = jnp.concatenate([tiles, jnp.zeros((1, sub, lanes), jnp.bfloat16)], axis=0)
    index = jnp.broadcast_to(
        table.reshape(experts, 1, capacity), (experts, hidden_split, capacity)
    ).reshape(-1)
    outgoing = padded[index].reshape(devices, capacity * sub, lanes)
    arrived = lax.all_to_all(outgoing, ("dp", "expert"), 0, 0, tiled=True)
    produced = expert_block(
        arrived.reshape(devices * capacity, sub, lanes), gate_weight, up_weight, down_weight
    )
    returned = lax.all_to_all(
        produced.reshape(devices, capacity * sub, lanes), ("dp", "expert"), 0, 0, tiled=True
    )
    pieces = returned.reshape(experts, hidden_split, capacity, sub, lanes)[chosen, :, slots]
    blended = jnp.sum(pieces.astype(jnp.float32), axis=1) * expert_mix.reshape(-1)[:, None, None]
    expert_update = (
        jnp.sum(blended.reshape(tok_rows, TOP, sub, lanes), axis=1)
        .reshape(tok_rows, width)
        .astype(jnp.bfloat16)
    )
    return (attention_update, expert_update)


def solution(mesh):
    in_specs = (
        P(("dp", "expert"), None),
        P(),
        P(None, "expert"),
        P(None, "expert"),
        P(None, "expert"),
        P("expert", None),
        P("dp", None, "expert"),
        P("dp", None, "expert"),
        P("dp", None),
        P("dp"),
        P("dp"),
        P(),
        P(("dp", "expert"), None),
        P(("dp", "expert"), None),
        P(("dp", "expert"), None, None),
        P(("dp", "expert"), None, None),
        P(("dp", "expert"), None, None),
    )
    out_specs = (P(("dp", "expert"), None), P(("dp", "expert"), None))
    return jax.shard_map(
        per_device, mesh=mesh, in_specs=in_specs, out_specs=out_specs, check_vma=False
    )
```

```python
import math

import jax
import jax.numpy as jnp
from jax import lax
from jax.sharding import PartitionSpec as P

HD = 128
FF = 1024
TOP = 8
GSIZE = 16
SB = 32


epsilon = 1e-06


def rms_scale(values, gain):
    widened = values.astype(jnp.float32)
    spread = jnp.mean(widened * widened, axis=-1, keepdims=True)
    return (widened * lax.rsqrt(spread + epsilon) * gain).astype(jnp.bfloat16)


def expert_block(block, gate_weight, up_weight, down_weight):
    rows, sub, lanes = block.shape
    gate = gate_weight[0].reshape(sub, lanes, -1)
    up = up_weight[0].reshape(sub, lanes, -1)
    contract = (((1, 2), (0, 1)), ((), ()))
    gated = lax.dot_general(block, gate, contract, preferred_element_type=jnp.float32)
    lifted = lax.dot_general(block, up, contract, preferred_element_type=jnp.float32)
    hidden = (jax.nn.silu(gated) * lifted).astype(jnp.bfloat16)
    produced = jnp.dot(hidden, down_weight[0], preferred_element_type=jnp.float32)
    return produced.astype(jnp.bfloat16).reshape(rows, sub, lanes)


def ring_shift(block, side, along_x, step):
    pairs = []
    for source in range(side * side):
        row, column = divmod(source, side)
        if along_x:
            target = ((row + step) % side) * side + column
        else:
            target = row * side + (column + step) % side
        pairs.append((source, target))
    return lax.ppermute(block, "expert", pairs)


def ring_gather(block, side, along_x):
    assert side == 4
    from_left = ring_shift(block, side, along_x, 1)
    from_right = ring_shift(block, side, along_x, -1)
    cut = block.shape[-2] // 2
    far = jnp.concatenate(
        [
            ring_shift(from_left[..., :cut, :], side, along_x, 1),
            ring_shift(from_right[..., cut:, :], side, along_x, -1),
        ],
        axis=-2,
    )
    return jnp.stack([block, from_right, far, from_left])


def ring_reduce(relative, side, along_x):
    assert side == 4
    cut = relative.shape[-2] // 2
    far = relative[2].astype(jnp.bfloat16)
    came_left = ring_shift(far[..., :cut, :], side, along_x, 1).astype(jnp.float32)
    came_right = ring_shift(far[..., cut:, :], side, along_x, -1).astype(jnp.float32)
    spare = [(0, 0)] * (relative.ndim - 3)
    rightward = relative[1] + jnp.pad(came_left, spare + [(0, cut), (0, 0)])
    leftward = relative[3] + jnp.pad(came_right, spare + [(cut, 0), (0, 0)])
    from_left = ring_shift(rightward.astype(jnp.bfloat16), side, along_x, 1)
    from_right = ring_shift(leftward.astype(jnp.bfloat16), side, along_x, -1)
    return relative[0] + from_left.astype(jnp.float32) + from_right.astype(jnp.float32)


def per_device(
    residual_in,
    attention_gain,
    query_weight,
    key_weight,
    value_weight,
    output_weight,
    prompt_keys,
    prompt_values,
    group_index,
    prompt_length,
    own_length,
    expert_gain,
    expert_ids,
    expert_mix,
    gate_weight,
    up_weight,
    down_weight,
):
    tok_rows, width = residual_in.shape
    local_width = query_weight.shape[1]
    heads_here = local_width // HD
    requests = group_index.shape[1]
    longest = prompt_keys.shape[1]
    groups_here = prompt_keys.shape[0]
    normed = rms_scale(residual_in, attention_gain)
    expert_groups = lax.axis_size("expert")
    side = math.isqrt(expert_groups)
    half = tok_rows // 2
    first = ring_gather(normed[:half], side, True)
    second = ring_gather(normed[half:], side, False)
    first = ring_gather(first, side, False)
    second = ring_gather(second, side, True)
    joined = jnp.concatenate([query_weight, key_weight, value_weight], axis=1)
    first = jnp.dot(first.reshape(-1, width), joined, preferred_element_type=jnp.float32)
    second = jnp.dot(second.reshape(-1, width), joined, preferred_element_type=jnp.float32)
    first = jnp.swapaxes(first.astype(jnp.bfloat16).reshape(side, side, half, -1), 0, 1)
    second = second.astype(jnp.bfloat16).reshape(side, side, half, -1)
    relative = jnp.concatenate([first, second], axis=2)
    place = lax.axis_index("expert")
    offsets = jnp.arange(side, dtype=jnp.int32)
    across = (offsets - place // side) % side
    down = (offsets - place % side) % side
    projected = relative[across][:, down].reshape(expert_groups * tok_rows, -1)
    layout = (requests, SB, heads_here, HD)
    queries = projected[:, :local_width].reshape(layout)
    new_keys = projected[:, local_width : 2 * local_width].reshape(layout)
    new_values = projected[:, 2 * local_width :].reshape(layout)
    scale = HD ** (-0.5)
    positions = jnp.arange(SB, dtype=jnp.int32)
    own_scores = (
        jnp.einsum("rihd,rjhd->rhij", queries, new_keys, preferred_element_type=jnp.float32) * scale
    )
    own_scores = jnp.where(
        positions[None, None, None, :] < own_length[:, None, None, None], own_scores, -jnp.inf
    )
    member = group_index[0]
    prompt_positions = jnp.arange(longest, dtype=jnp.int32)

    def group_step(group, attended):
        first = jnp.sum((member < group).astype(jnp.int32))
        start = jnp.minimum(first, requests - GSIZE)
        window_queries = lax.dynamic_slice_in_dim(queries, start, GSIZE, 0)
        group_keys = lax.dynamic_index_in_dim(prompt_keys, group, 0, keepdims=False).reshape(
            longest, heads_here, HD
        )
        group_values = lax.dynamic_index_in_dim(prompt_values, group, 0, keepdims=False).reshape(
            longest, heads_here, HD
        )
        scores = (
            jnp.einsum(
                "rihd,jhd->rhij", window_queries, group_keys, preferred_element_type=jnp.float32
            )
            * scale
        )
        limit = lax.dynamic_index_in_dim(prompt_length, group, 0, keepdims=False)
        scores = jnp.where(prompt_positions < limit, scores, -jnp.inf)
        window_own = lax.dynamic_slice_in_dim(own_scores, start, GSIZE, 0)
        highest = jnp.maximum(jnp.max(scores, axis=-1), jnp.max(window_own, axis=-1))
        prompt_weights = jnp.exp(scores - highest[..., None]).astype(jnp.bfloat16)
        own_weights = jnp.exp(window_own - highest[..., None]).astype(jnp.bfloat16)
        window_values = lax.dynamic_slice_in_dim(new_values, start, GSIZE, 0)
        summed = jnp.einsum(
            "rhij,jhd->rihd", prompt_weights, group_values, preferred_element_type=jnp.float32
        )
        summed = summed + jnp.einsum(
            "rhij,rjhd->rihd", own_weights, window_values, preferred_element_type=jnp.float32
        )
        totals = jnp.sum(prompt_weights, axis=-1, dtype=jnp.float32) + jnp.sum(
            own_weights, axis=-1, dtype=jnp.float32
        )
        result = (summed / jnp.transpose(totals, (0, 2, 1))[..., None]).astype(jnp.bfloat16)
        inside = lax.dynamic_slice_in_dim(member, start, GSIZE, 0) == group
        current = lax.dynamic_slice_in_dim(attended, start, GSIZE, 0)
        merged = jnp.where(inside[:, None, None, None], result, current)
        return lax.dynamic_update_slice_in_dim(attended, merged, start, 0)

    attended = lax.fori_loop(0, groups_here, group_step, jnp.zeros(layout, jnp.bfloat16))
    owners = attended.reshape(side, side, tok_rows, local_width)
    ahead_x = (offsets + place // side) % side
    ahead_y = (offsets + place % side) % side
    owners = owners[ahead_x][:, ahead_y]
    first = owners[:, :, :half].reshape(-1, local_width)
    second = jnp.swapaxes(owners[:, :, half:], 0, 1).reshape(-1, local_width)
    first = jnp.dot(first, output_weight, preferred_element_type=jnp.float32)
    second = jnp.dot(second, output_weight, preferred_element_type=jnp.float32)
    first = ring_reduce(first.reshape(side, side, half, width), side, True)
    second = ring_reduce(second.reshape(side, side, half, width), side, False)
    first = ring_reduce(first, side, False)
    second = ring_reduce(second, side, True)
    attention_update = jnp.concatenate([first, second], axis=0).astype(jnp.bfloat16)
    expert_input = rms_scale(
        residual_in.astype(jnp.float32) + attention_update.astype(jnp.float32), expert_gain
    )
    data_groups = lax.axis_size("dp")
    devices = data_groups * expert_groups
    hidden_split = FF // gate_weight.shape[2]
    experts = devices // hidden_split
    capacity = max(2, tok_rows * TOP * 3 // (2 * experts))
    chosen = expert_ids.reshape(-1)
    routes_here = chosen.shape[0]
    owners = jnp.arange(routes_here, dtype=jnp.int32) // TOP
    matches = (chosen[:, None] == jnp.arange(experts, dtype=jnp.int32)[None, :]).astype(jnp.int32)
    slots = jnp.sum((jnp.cumsum(matches, axis=0) - matches) * matches, axis=1)
    table = (
        jnp.full((experts * capacity,), tok_rows, jnp.int32)
        .at[chosen * capacity + slots]
        .set(owners)
    )
    lanes = 128
    sub = width // lanes
    tiles = expert_input.reshape(tok_rows, sub, lanes)
    padded = jnp.concatenate([tiles, jnp.zeros((1, sub, lanes), jnp.bfloat16)], axis=0)
    index = jnp.broadcast_to(
        table.reshape(experts, 1, capacity), (experts, hidden_split, capacity)
    ).reshape(-1)
    outgoing = padded[index].reshape(devices, capacity * sub, lanes)
    arrived = lax.all_to_all(outgoing, ("dp", "expert"), 0, 0, tiled=True)
    produced = expert_block(
        arrived.reshape(devices * capacity, sub, lanes), gate_weight, up_weight, down_weight
    )
    returned = lax.all_to_all(
        produced.reshape(devices, capacity * sub, lanes), ("dp", "expert"), 0, 0, tiled=True
    )
    returned = returned.reshape(devices * capacity, sub, lanes)
    spot = chosen * (hidden_split * capacity) + slots
    blended = returned[spot].astype(jnp.float32)
    for block in range(1, hidden_split):
        blended = blended + returned[spot + block * capacity].astype(jnp.float32)
    blended = blended * expert_mix.reshape(-1)[:, None, None]
    expert_update = (
        jnp.sum(blended.reshape(tok_rows, TOP, sub, lanes), axis=1)
        .reshape(tok_rows, width)
        .astype(jnp.bfloat16)
    )
    return (attention_update, expert_update)


def solution(mesh):
    in_specs = (
        P(("dp", "expert"), None),
        P(),
        P(None, "expert"),
        P(None, "expert"),
        P(None, "expert"),
        P("expert", None),
        P("dp", None, "expert"),
        P("dp", None, "expert"),
        P("dp", None),
        P("dp"),
        P("dp"),
        P(),
        P(("dp", "expert"), None),
        P(("dp", "expert"), None),
        P(("dp", "expert"), None, None),
        P(("dp", "expert"), None, None),
        P(("dp", "expert"), None, None),
    )
    out_specs = (P(("dp", "expert"), None), P(("dp", "expert"), None))
    return jax.shard_map(
        per_device, mesh=mesh, in_specs=in_specs, out_specs=out_specs, check_vma=False
    )
```

```python
import math

import jax
import jax.numpy as jnp
from jax import lax
from jax.sharding import PartitionSpec as P

HD = 128
FF = 1024
TOP = 8
GSIZE = 16
SB = 32


epsilon = 1e-06


def rms_scale(values, gain):
    widened = values.astype(jnp.float32)
    spread = jnp.mean(widened * widened, axis=-1, keepdims=True)
    return (widened * lax.rsqrt(spread + epsilon) * gain).astype(jnp.bfloat16)


def expert_block(block, gate_weight, up_weight, down_weight):
    rows, sub, lanes = block.shape
    gate = gate_weight[0].reshape(sub, lanes, -1)
    up = up_weight[0].reshape(sub, lanes, -1)
    contract = (((1, 2), (0, 1)), ((), ()))
    gated = lax.dot_general(block, gate, contract, preferred_element_type=jnp.float32)
    lifted = lax.dot_general(block, up, contract, preferred_element_type=jnp.float32)
    hidden = (jax.nn.silu(gated) * lifted).astype(jnp.bfloat16)
    produced = jnp.dot(hidden, down_weight[0], preferred_element_type=jnp.float32)
    return produced.astype(jnp.bfloat16).reshape(rows, sub, lanes)


def ring_shift(block, side, along_x, step):
    pairs = []
    for source in range(side * side):
        row, column = divmod(source, side)
        if along_x:
            target = ((row + step) % side) * side + column
        else:
            target = row * side + (column + step) % side
        pairs.append((source, target))
    return lax.ppermute(block, "expert", pairs)


def ring_gather(block, side, along_x):
    assert side == 4
    from_left = ring_shift(block, side, along_x, 1)
    from_right = ring_shift(block, side, along_x, -1)
    cut = block.shape[-2] // 2
    far = jnp.concatenate(
        [
            ring_shift(from_left[..., :cut, :], side, along_x, 1),
            ring_shift(from_right[..., cut:, :], side, along_x, -1),
        ],
        axis=-2,
    )
    return jnp.stack([block, from_right, far, from_left])


def ring_reduce(relative, side, along_x):
    assert side == 4
    cut = relative.shape[-2] // 2
    far = relative[2].astype(jnp.bfloat16)
    came_left = ring_shift(far[..., :cut, :], side, along_x, 1).astype(jnp.float32)
    came_right = ring_shift(far[..., cut:, :], side, along_x, -1).astype(jnp.float32)
    rightward = jnp.concatenate([relative[1][..., :cut, :] + came_left, relative[1][..., cut:, :]], axis=-2)
    leftward = jnp.concatenate([relative[3][..., :cut, :], relative[3][..., cut:, :] + came_right], axis=-2)
    from_left = ring_shift(rightward.astype(jnp.bfloat16), side, along_x, 1)
    from_right = ring_shift(leftward.astype(jnp.bfloat16), side, along_x, -1)
    return relative[0] + from_left.astype(jnp.float32) + from_right.astype(jnp.float32)


def per_device(
    residual_in,
    attention_gain,
    query_weight,
    key_weight,
    value_weight,
    output_weight,
    prompt_keys,
    prompt_values,
    group_index,
    prompt_length,
    own_length,
    expert_gain,
    expert_ids,
    expert_mix,
    gate_weight,
    up_weight,
    down_weight,
):
    tok_rows, width = residual_in.shape
    local_width = query_weight.shape[1]
    heads_here = local_width // HD
    requests = group_index.shape[1]
    longest = prompt_keys.shape[1]
    groups_here = prompt_keys.shape[0]
    normed = rms_scale(residual_in, attention_gain)
    expert_groups = lax.axis_size("expert")
    side = math.isqrt(expert_groups)
    half = tok_rows // 2
    first = ring_gather(normed[:half], side, True)
    second = ring_gather(normed[half:], side, False)
    first = ring_gather(first, side, False)
    second = ring_gather(second, side, True)
    joined = jnp.concatenate([query_weight, key_weight, value_weight], axis=1)
    first = jnp.dot(first.reshape(-1, width), joined, preferred_element_type=jnp.float32)
    second = jnp.dot(second.reshape(-1, width), joined, preferred_element_type=jnp.float32)
    first = jnp.swapaxes(first.astype(jnp.bfloat16).reshape(side, side, half, -1), 0, 1)
    second = second.astype(jnp.bfloat16).reshape(side, side, half, -1)
    relative = jnp.concatenate([first, second], axis=2)
    place = lax.axis_index("expert")
    offsets = jnp.arange(side, dtype=jnp.int32)
    across = (offsets - place // side) % side
    down = (offsets - place % side) % side
    projected = relative[across][:, down].reshape(expert_groups * tok_rows, -1)
    layout = (requests, SB, heads_here, HD)
    queries = projected[:, :local_width].reshape(layout)
    new_keys = projected[:, local_width : 2 * local_width].reshape(layout)
    new_values = projected[:, 2 * local_width :].reshape(layout)
    scale = HD ** (-0.5)
    positions = jnp.arange(SB, dtype=jnp.int32)
    own_scores = (
        jnp.einsum("rihd,rjhd->rhij", queries, new_keys, preferred_element_type=jnp.float32) * scale
    )
    own_scores = jnp.where(
        positions[None, None, None, :] < own_length[:, None, None, None], own_scores, -jnp.inf
    )
    member = group_index[0]
    prompt_positions = jnp.arange(longest, dtype=jnp.int32)

    def group_step(group, attended):
        first = jnp.sum((member < group).astype(jnp.int32))
        start = jnp.minimum(first, requests - GSIZE)
        window_queries = lax.dynamic_slice_in_dim(queries, start, GSIZE, 0)
        group_keys = lax.dynamic_index_in_dim(prompt_keys, group, 0, keepdims=False).reshape(
            longest, heads_here, HD
        )
        group_values = lax.dynamic_index_in_dim(prompt_values, group, 0, keepdims=False).reshape(
            longest, heads_here, HD
        )
        scores = (
            jnp.dot(
                window_queries.reshape(GSIZE * SB, local_width),
                group_keys.reshape(longest, local_width).T,
                preferred_element_type=jnp.float32,
            ).reshape(GSIZE, SB, heads_here, longest)
            * scale
        )
        scores = jnp.transpose(scores, (0, 2, 1, 3))
        limit = lax.dynamic_index_in_dim(prompt_length, group, 0, keepdims=False)
        scores = jnp.where(prompt_positions < limit, scores, -jnp.inf)
        window_own = lax.dynamic_slice_in_dim(own_scores, start, GSIZE, 0)
        highest = jnp.maximum(jnp.max(scores, axis=-1), jnp.max(window_own, axis=-1))
        prompt_weights = jnp.exp(scores - highest[..., None]).astype(jnp.bfloat16)
        own_weights = jnp.exp(window_own - highest[..., None]).astype(jnp.bfloat16)
        window_values = lax.dynamic_slice_in_dim(new_values, start, GSIZE, 0)
        summed = jnp.dot(
            jnp.transpose(prompt_weights, (0, 2, 1, 3)).reshape(GSIZE * SB, longest),
            group_values.reshape(longest, local_width),
            preferred_element_type=jnp.float32,
        ).reshape(GSIZE, SB, heads_here, HD)
        summed = summed + jnp.einsum(
            "rhij,rjhd->rihd", own_weights, window_values, preferred_element_type=jnp.float32
        )
        totals = jnp.sum(prompt_weights, axis=-1, dtype=jnp.float32) + jnp.sum(
            own_weights, axis=-1, dtype=jnp.float32
        )
        result = (summed / jnp.transpose(totals, (0, 2, 1))[..., None]).astype(jnp.bfloat16)
        inside = lax.dynamic_slice_in_dim(member, start, GSIZE, 0) == group
        current = lax.dynamic_slice_in_dim(attended, start, GSIZE, 0)
        merged = jnp.where(inside[:, None, None, None], result, current)
        return lax.dynamic_update_slice_in_dim(attended, merged, start, 0)

    attended = lax.fori_loop(0, groups_here, group_step, jnp.zeros(layout, jnp.bfloat16))
    owners = attended.reshape(side, side, tok_rows, local_width)
    ahead_x = (offsets + place // side) % side
    ahead_y = (offsets + place % side) % side
    owners = owners[ahead_x][:, ahead_y]
    first = owners[:, :, :half].reshape(-1, local_width)
    second = jnp.swapaxes(owners[:, :, half:], 0, 1).reshape(-1, local_width)
    first = jnp.dot(first, output_weight, preferred_element_type=jnp.float32)
    second = jnp.dot(second, output_weight, preferred_element_type=jnp.float32)
    first = ring_reduce(first.reshape(side, side, half, width), side, True)
    second = ring_reduce(second.reshape(side, side, half, width), side, False)
    first = ring_reduce(first, side, False)
    second = ring_reduce(second, side, True)
    attention_update = jnp.concatenate([first, second], axis=0).astype(jnp.bfloat16)
    expert_input = rms_scale(
        residual_in.astype(jnp.float32) + attention_update.astype(jnp.float32), expert_gain
    )
    data_groups = lax.axis_size("dp")
    devices = data_groups * expert_groups
    hidden_split = FF // gate_weight.shape[2]
    experts = devices // hidden_split
    capacity = max(2, tok_rows * TOP * 3 // (2 * experts))
    chosen = expert_ids.reshape(-1)
    routes_here = chosen.shape[0]
    owners = jnp.arange(routes_here, dtype=jnp.int32) // TOP
    matches = (chosen[:, None] == jnp.arange(experts, dtype=jnp.int32)[None, :]).astype(jnp.int32)
    slots = jnp.sum((jnp.cumsum(matches, axis=0) - matches) * matches, axis=1)
    table = (
        jnp.full((experts * capacity,), tok_rows, jnp.int32)
        .at[chosen * capacity + slots]
        .set(owners)
    )
    lanes = 128
    sub = width // lanes
    tiles = expert_input.reshape(tok_rows, sub, lanes)
    padded = jnp.concatenate([tiles, jnp.zeros((1, sub, lanes), jnp.bfloat16)], axis=0)
    index = jnp.broadcast_to(
        table.reshape(experts, 1, capacity), (experts, hidden_split, capacity)
    ).reshape(-1)
    outgoing = padded[index].reshape(devices, capacity * sub, lanes)
    arrived = lax.all_to_all(outgoing, ("dp", "expert"), 0, 0, tiled=True)
    produced = expert_block(
        arrived.reshape(devices * capacity, sub, lanes), gate_weight, up_weight, down_weight
    )
    returned = lax.all_to_all(
        produced.reshape(devices, capacity * sub, lanes), ("dp", "expert"), 0, 0, tiled=True
    )
    pieces = returned.reshape(experts, hidden_split, capacity, sub, lanes)[chosen, :, slots]
    blended = jnp.sum(pieces.astype(jnp.float32), axis=1) * expert_mix.reshape(-1)[:, None, None]
    expert_update = (
        jnp.sum(blended.reshape(tok_rows, TOP, sub, lanes), axis=1)
        .reshape(tok_rows, width)
        .astype(jnp.bfloat16)
    )
    return (attention_update, expert_update)


def solution(mesh):
    in_specs = (
        P(("dp", "expert"), None),
        P(),
        P(None, "expert"),
        P(None, "expert"),
        P(None, "expert"),
        P("expert", None),
        P("dp", None, "expert"),
        P("dp", None, "expert"),
        P("dp", None),
        P("dp"),
        P("dp"),
        P(),
        P(("dp", "expert"), None),
        P(("dp", "expert"), None),
        P(("dp", "expert"), None, None),
        P(("dp", "expert"), None, None),
        P(("dp", "expert"), None, None),
    )
    out_specs = (P(("dp", "expert"), None), P(("dp", "expert"), None))
    return jax.shard_map(
        per_device, mesh=mesh, in_specs=in_specs, out_specs=out_specs, check_vma=False
    )
```

```python
import math

import jax
import jax.numpy as jnp
from jax import lax
from jax.sharding import PartitionSpec as P

HD = 128
FF = 1024
TOP = 8
GSIZE = 16
SB = 32


epsilon = 1e-06


def rms_scale(values, gain):
    widened = values.astype(jnp.float32)
    spread = jnp.mean(widened * widened, axis=-1, keepdims=True)
    return (widened * lax.rsqrt(spread + epsilon) * gain).astype(jnp.bfloat16)


def expert_block(block, gate_weight, up_weight, down_weight):
    rows, sub, lanes = block.shape
    gate = gate_weight[0].reshape(sub, lanes, -1)
    up = up_weight[0].reshape(sub, lanes, -1)
    contract = (((1, 2), (0, 1)), ((), ()))
    gated = lax.dot_general(block, gate, contract, preferred_element_type=jnp.float32)
    lifted = lax.dot_general(block, up, contract, preferred_element_type=jnp.float32)
    hidden = (jax.nn.silu(gated) * lifted).astype(jnp.bfloat16)
    produced = jnp.dot(hidden, down_weight[0], preferred_element_type=jnp.float32)
    return produced.astype(jnp.bfloat16).reshape(rows, sub, lanes)


def ring_shift(block, side, along_x, step):
    pairs = []
    for source in range(side * side):
        row, column = divmod(source, side)
        if along_x:
            target = ((row + step) % side) * side + column
        else:
            target = row * side + (column + step) % side
        pairs.append((source, target))
    return lax.ppermute(block, "expert", pairs)


def ring_gather(block, side, along_x, split=True):
    assert side == 4
    from_left = ring_shift(block, side, along_x, 1)
    from_right = ring_shift(block, side, along_x, -1)
    cut = block.shape[-2] // 2
    if not split:
        far = ring_shift(from_left, side, along_x, 1)
        return jnp.stack([block, from_right, far, from_left])
    far = jnp.concatenate(
        [
            ring_shift(from_left[..., :cut, :], side, along_x, 1),
            ring_shift(from_right[..., cut:, :], side, along_x, -1),
        ],
        axis=-2,
    )
    return jnp.stack([block, from_right, far, from_left])


def ring_reduce(relative, side, along_x, split=True):
    assert side == 4
    cut = relative.shape[-2] // 2
    if not split:
        came_left = ring_shift(relative[2].astype(jnp.bfloat16), side, along_x, 1)
        rightward = relative[1] + came_left.astype(jnp.float32)
        from_left = ring_shift(rightward.astype(jnp.bfloat16), side, along_x, 1)
        from_right = ring_shift(relative[3].astype(jnp.bfloat16), side, along_x, -1)
        return relative[0] + from_left.astype(jnp.float32) + from_right.astype(jnp.float32)
    far = relative[2].astype(jnp.bfloat16)
    came_left = ring_shift(far[..., :cut, :], side, along_x, 1).astype(jnp.float32)
    came_right = ring_shift(far[..., cut:, :], side, along_x, -1).astype(jnp.float32)
    rightward = jnp.concatenate([relative[1][..., :cut, :] + came_left, relative[1][..., cut:, :]], axis=-2)
    leftward = jnp.concatenate([relative[3][..., :cut, :], relative[3][..., cut:, :] + came_right], axis=-2)
    from_left = ring_shift(rightward.astype(jnp.bfloat16), side, along_x, 1)
    from_right = ring_shift(leftward.astype(jnp.bfloat16), side, along_x, -1)
    return relative[0] + from_left.astype(jnp.float32) + from_right.astype(jnp.float32)


def per_device(
    residual_in,
    attention_gain,
    query_weight,
    key_weight,
    value_weight,
    output_weight,
    prompt_keys,
    prompt_values,
    group_index,
    prompt_length,
    own_length,
    expert_gain,
    expert_ids,
    expert_mix,
    gate_weight,
    up_weight,
    down_weight,
):
    tok_rows, width = residual_in.shape
    local_width = query_weight.shape[1]
    heads_here = local_width // HD
    requests = group_index.shape[1]
    longest = prompt_keys.shape[1]
    groups_here = prompt_keys.shape[0]
    normed = rms_scale(residual_in, attention_gain)
    expert_groups = lax.axis_size("expert")
    side = math.isqrt(expert_groups)
    half = tok_rows // 2
    first = ring_gather(normed[:half], side, True, False)
    second = ring_gather(normed[half:], side, False, False)
    first = ring_gather(first, side, False)
    second = ring_gather(second, side, True)
    joined = jnp.concatenate([query_weight, key_weight, value_weight], axis=1)
    first = jnp.dot(first.reshape(-1, width), joined, preferred_element_type=jnp.float32)
    second = jnp.dot(second.reshape(-1, width), joined, preferred_element_type=jnp.float32)
    first = jnp.swapaxes(first.astype(jnp.bfloat16).reshape(side, side, half, -1), 0, 1)
    second = second.astype(jnp.bfloat16).reshape(side, side, half, -1)
    relative = jnp.concatenate([first, second], axis=2)
    place = lax.axis_index("expert")
    offsets = jnp.arange(side, dtype=jnp.int32)
    across = (offsets - place // side) % side
    down = (offsets - place % side) % side
    projected = relative[across][:, down].reshape(expert_groups * tok_rows, -1)
    layout = (requests, SB, heads_here, HD)
    queries = projected[:, :local_width].reshape(layout)
    new_keys = projected[:, local_width : 2 * local_width].reshape(layout)
    new_values = projected[:, 2 * local_width :].reshape(layout)
    scale = HD ** (-0.5)
    positions = jnp.arange(SB, dtype=jnp.int32)
    own_scores = (
        jnp.einsum("rihd,rjhd->rhij", queries, new_keys, preferred_element_type=jnp.float32) * scale
    )
    own_scores = jnp.where(
        positions[None, None, None, :] < own_length[:, None, None, None], own_scores, -jnp.inf
    )
    member = group_index[0]
    prompt_positions = jnp.arange(longest, dtype=jnp.int32)

    def group_step(group, attended):
        first = jnp.sum((member < group).astype(jnp.int32))
        start = jnp.minimum(first, requests - GSIZE)
        window_queries = lax.dynamic_slice_in_dim(queries, start, GSIZE, 0)
        group_keys = lax.dynamic_index_in_dim(prompt_keys, group, 0, keepdims=False).reshape(
            longest, heads_here, HD
        )
        group_values = lax.dynamic_index_in_dim(prompt_values, group, 0, keepdims=False).reshape(
            longest, heads_here, HD
        )
        scores = (
            jnp.einsum(
                "rihd,jhd->rhij", window_queries, group_keys, preferred_element_type=jnp.float32
            )
            * scale
        )
        limit = lax.dynamic_index_in_dim(prompt_length, group, 0, keepdims=False)
        scores = jnp.where(prompt_positions < limit, scores, -jnp.inf)
        window_own = lax.dynamic_slice_in_dim(own_scores, start, GSIZE, 0)
        highest = jnp.maximum(jnp.max(scores, axis=-1), jnp.max(window_own, axis=-1))
        prompt_weights = jnp.exp(scores - highest[..., None]).astype(jnp.bfloat16)
        own_weights = jnp.exp(window_own - highest[..., None]).astype(jnp.bfloat16)
        window_values = lax.dynamic_slice_in_dim(new_values, start, GSIZE, 0)
        summed = jnp.einsum(
            "rhij,jhd->rihd", prompt_weights, group_values, preferred_element_type=jnp.float32
        )
        summed = summed + jnp.einsum(
            "rhij,rjhd->rihd", own_weights, window_values, preferred_element_type=jnp.float32
        )
        totals = jnp.sum(prompt_weights, axis=-1, dtype=jnp.float32) + jnp.sum(
            own_weights, axis=-1, dtype=jnp.float32
        )
        result = (summed / jnp.transpose(totals, (0, 2, 1))[..., None]).astype(jnp.bfloat16)
        inside = lax.dynamic_slice_in_dim(member, start, GSIZE, 0) == group
        current = lax.dynamic_slice_in_dim(attended, start, GSIZE, 0)
        merged = jnp.where(inside[:, None, None, None], result, current)
        return lax.dynamic_update_slice_in_dim(attended, merged, start, 0)

    attended = lax.fori_loop(0, groups_here, group_step, jnp.zeros(layout, jnp.bfloat16))
    owners = attended.reshape(side, side, tok_rows, local_width)
    ahead_x = (offsets + place // side) % side
    ahead_y = (offsets + place % side) % side
    owners = owners[ahead_x][:, ahead_y]
    first = owners[:, :, :half].reshape(-1, local_width)
    second = jnp.swapaxes(owners[:, :, half:], 0, 1).reshape(-1, local_width)
    first = jnp.dot(first, output_weight, preferred_element_type=jnp.float32)
    second = jnp.dot(second, output_weight, preferred_element_type=jnp.float32)
    first = ring_reduce(first.reshape(side, side, half, width), side, True)
    second = ring_reduce(second.reshape(side, side, half, width), side, False)
    first = ring_reduce(first, side, False, False)
    second = ring_reduce(second, side, True, False)
    attention_update = jnp.concatenate([first, second], axis=0).astype(jnp.bfloat16)
    expert_input = rms_scale(
        residual_in.astype(jnp.float32) + attention_update.astype(jnp.float32), expert_gain
    )
    data_groups = lax.axis_size("dp")
    devices = data_groups * expert_groups
    hidden_split = FF // gate_weight.shape[2]
    experts = devices // hidden_split
    capacity = max(2, tok_rows * TOP * 3 // (2 * experts))
    chosen = expert_ids.reshape(-1)
    routes_here = chosen.shape[0]
    owners = jnp.arange(routes_here, dtype=jnp.int32) // TOP
    matches = (chosen[:, None] == jnp.arange(experts, dtype=jnp.int32)[None, :]).astype(jnp.int32)
    slots = jnp.sum((jnp.cumsum(matches, axis=0) - matches) * matches, axis=1)
    table = (
        jnp.full((experts * capacity,), tok_rows, jnp.int32)
        .at[chosen * capacity + slots]
        .set(owners)
    )
    lanes = 128
    sub = width // lanes
    tiles = expert_input.reshape(tok_rows, sub, lanes)
    padded = jnp.concatenate([tiles, jnp.zeros((1, sub, lanes), jnp.bfloat16)], axis=0)
    index = jnp.broadcast_to(
        table.reshape(experts, 1, capacity), (experts, hidden_split, capacity)
    ).reshape(-1)
    outgoing = padded[index].reshape(devices, capacity * sub, lanes)
    arrived = lax.all_to_all(outgoing, ("dp", "expert"), 0, 0, tiled=True)
    produced = expert_block(
        arrived.reshape(devices * capacity, sub, lanes), gate_weight, up_weight, down_weight
    )
    returned = lax.all_to_all(
        produced.reshape(devices, capacity * sub, lanes), ("dp", "expert"), 0, 0, tiled=True
    )
    pieces = returned.reshape(experts, hidden_split, capacity, sub, lanes)[chosen, :, slots]
    blended = jnp.sum(pieces.astype(jnp.float32), axis=1) * expert_mix.reshape(-1)[:, None, None]
    expert_update = (
        jnp.sum(blended.reshape(tok_rows, TOP, sub, lanes), axis=1)
        .reshape(tok_rows, width)
        .astype(jnp.bfloat16)
    )
    return (attention_update, expert_update)


def solution(mesh):
    in_specs = (
        P(("dp", "expert"), None),
        P(),
        P(None, "expert"),
        P(None, "expert"),
        P(None, "expert"),
        P("expert", None),
        P("dp", None, "expert"),
        P("dp", None, "expert"),
        P("dp", None),
        P("dp"),
        P("dp"),
        P(),
        P(("dp", "expert"), None),
        P(("dp", "expert"), None),
        P(("dp", "expert"), None, None),
        P(("dp", "expert"), None, None),
        P(("dp", "expert"), None, None),
    )
    out_specs = (P(("dp", "expert"), None), P(("dp", "expert"), None))
    return jax.shard_map(
        per_device, mesh=mesh, in_specs=in_specs, out_specs=out_specs, check_vma=False
    )
```

```python
import math

import jax
import jax.numpy as jnp
from jax import lax
from jax.sharding import PartitionSpec as P

HD = 128
FF = 1024
TOP = 8
GSIZE = 16
SB = 32


epsilon = 1e-06


def rms_scale(values, gain):
    widened = values.astype(jnp.float32)
    spread = jnp.mean(widened * widened, axis=-1, keepdims=True)
    return (widened * lax.rsqrt(spread + epsilon) * gain).astype(jnp.bfloat16)


def expert_block(block, gate_weight, up_weight, down_weight):
    rows, sub, lanes = block.shape
    gate = gate_weight[0].reshape(sub, lanes, -1)
    up = up_weight[0].reshape(sub, lanes, -1)
    contract = (((1, 2), (0, 1)), ((), ()))
    gated = lax.dot_general(block, gate, contract, preferred_element_type=jnp.float32)
    lifted = lax.dot_general(block, up, contract, preferred_element_type=jnp.float32)
    hidden = (jax.nn.silu(gated) * lifted).astype(jnp.bfloat16)
    produced = jnp.dot(hidden, down_weight[0], preferred_element_type=jnp.float32)
    return produced.astype(jnp.bfloat16).reshape(rows, sub, lanes)


def ring_shift(block, side, along_x, step):
    pairs = []
    for source in range(side * side):
        row, column = divmod(source, side)
        if along_x:
            target = ((row + step) % side) * side + column
        else:
            target = row * side + (column + step) % side
        pairs.append((source, target))
    return lax.ppermute(block, "expert", pairs)


def ring_gather(block, side, along_x, split=True, stacked=True):
    assert side == 4
    from_left = ring_shift(block, side, along_x, 1)
    from_right = ring_shift(block, side, along_x, -1)
    cut = block.shape[-2] // 2
    if not split:
        far = ring_shift(from_left, side, along_x, 1)
        return jnp.stack([block, from_right, far, from_left])
    far = jnp.concatenate(
        [
            ring_shift(from_left[..., :cut, :], side, along_x, 1),
            ring_shift(from_right[..., cut:, :], side, along_x, -1),
        ],
        axis=-2,
    )
    if not stacked:
        return [block, from_right, far, from_left]
    return jnp.stack([block, from_right, far, from_left])


def ring_reduce(relative, side, along_x, split=True):
    assert side == 4
    cut = relative.shape[-2] // 2
    if not split:
        came_left = ring_shift(relative[2].astype(jnp.bfloat16), side, along_x, 1)
        rightward = relative[1] + came_left.astype(jnp.float32)
        from_left = ring_shift(rightward.astype(jnp.bfloat16), side, along_x, 1)
        from_right = ring_shift(relative[3].astype(jnp.bfloat16), side, along_x, -1)
        return relative[0] + from_left.astype(jnp.float32) + from_right.astype(jnp.float32)
    far = relative[2].astype(jnp.bfloat16)
    came_left = ring_shift(far[..., :cut, :], side, along_x, 1).astype(jnp.float32)
    came_right = ring_shift(far[..., cut:, :], side, along_x, -1).astype(jnp.float32)
    rightward = jnp.concatenate([relative[1][..., :cut, :] + came_left, relative[1][..., cut:, :]], axis=-2)
    leftward = jnp.concatenate([relative[3][..., :cut, :], relative[3][..., cut:, :] + came_right], axis=-2)
    from_left = ring_shift(rightward.astype(jnp.bfloat16), side, along_x, 1)
    from_right = ring_shift(leftward.astype(jnp.bfloat16), side, along_x, -1)
    return relative[0] + from_left.astype(jnp.float32) + from_right.astype(jnp.float32)


def per_device(
    residual_in,
    attention_gain,
    query_weight,
    key_weight,
    value_weight,
    output_weight,
    prompt_keys,
    prompt_values,
    group_index,
    prompt_length,
    own_length,
    expert_gain,
    expert_ids,
    expert_mix,
    gate_weight,
    up_weight,
    down_weight,
):
    tok_rows, width = residual_in.shape
    local_width = query_weight.shape[1]
    heads_here = local_width // HD
    requests = group_index.shape[1]
    longest = prompt_keys.shape[1]
    groups_here = prompt_keys.shape[0]
    normed = rms_scale(residual_in, attention_gain)
    expert_groups = lax.axis_size("expert")
    side = math.isqrt(expert_groups)
    half = tok_rows // 2
    first = ring_gather(normed[:half], side, True, False)
    second = ring_gather(normed[half:], side, False, False)
    joined = jnp.concatenate([query_weight, key_weight, value_weight], axis=1)

    def project(pieces):
        return jnp.stack(
            [
                jnp.dot(piece.reshape(-1, width), joined, preferred_element_type=jnp.float32)
                .astype(jnp.bfloat16)
                .reshape(side, half, -1)
                for piece in pieces
            ]
        )

    first = jnp.swapaxes(project(ring_gather(first, side, False, True, False)), 0, 1)
    second = project(ring_gather(second, side, True, True, False))
    relative = jnp.concatenate([first, second], axis=2)
    place = lax.axis_index("expert")
    offsets = jnp.arange(side, dtype=jnp.int32)
    across = (offsets - place // side) % side
    down = (offsets - place % side) % side
    projected = relative[across][:, down].reshape(expert_groups * tok_rows, -1)
    layout = (requests, SB, heads_here, HD)
    queries = projected[:, :local_width].reshape(layout)
    new_keys = projected[:, local_width : 2 * local_width].reshape(layout)
    new_values = projected[:, 2 * local_width :].reshape(layout)
    scale = HD ** (-0.5)
    positions = jnp.arange(SB, dtype=jnp.int32)
    own_scores = (
        jnp.einsum("rihd,rjhd->rhij", queries, new_keys, preferred_element_type=jnp.float32) * scale
    )
    own_scores = jnp.where(
        positions[None, None, None, :] < own_length[:, None, None, None], own_scores, -jnp.inf
    )
    member = group_index[0]
    prompt_positions = jnp.arange(longest, dtype=jnp.int32)

    def group_step(group, attended):
        first = jnp.sum((member < group).astype(jnp.int32))
        start = jnp.minimum(first, requests - GSIZE)
        window_queries = lax.dynamic_slice_in_dim(queries, start, GSIZE, 0)
        group_keys = lax.dynamic_index_in_dim(prompt_keys, group, 0, keepdims=False).reshape(
            longest, heads_here, HD
        )
        group_values = lax.dynamic_index_in_dim(prompt_values, group, 0, keepdims=False).reshape(
            longest, heads_here, HD
        )
        scores = (
            jnp.einsum(
                "rihd,jhd->rhij", window_queries, group_keys, preferred_element_type=jnp.float32
            )
            * scale
        )
        limit = lax.dynamic_index_in_dim(prompt_length, group, 0, keepdims=False)
        scores = jnp.where(prompt_positions < limit, scores, -jnp.inf)
        window_own = lax.dynamic_slice_in_dim(own_scores, start, GSIZE, 0)
        highest = jnp.maximum(jnp.max(scores, axis=-1), jnp.max(window_own, axis=-1))
        prompt_weights = jnp.exp(scores - highest[..., None]).astype(jnp.bfloat16)
        own_weights = jnp.exp(window_own - highest[..., None]).astype(jnp.bfloat16)
        window_values = lax.dynamic_slice_in_dim(new_values, start, GSIZE, 0)
        summed = jnp.einsum(
            "rhij,jhd->rihd", prompt_weights, group_values, preferred_element_type=jnp.float32
        )
        summed = summed + jnp.einsum(
            "rhij,rjhd->rihd", own_weights, window_values, preferred_element_type=jnp.float32
        )
        totals = jnp.sum(prompt_weights, axis=-1, dtype=jnp.float32) + jnp.sum(
            own_weights, axis=-1, dtype=jnp.float32
        )
        result = (summed / jnp.transpose(totals, (0, 2, 1))[..., None]).astype(jnp.bfloat16)
        inside = lax.dynamic_slice_in_dim(member, start, GSIZE, 0) == group
        current = lax.dynamic_slice_in_dim(attended, start, GSIZE, 0)
        merged = jnp.where(inside[:, None, None, None], result, current)
        return lax.dynamic_update_slice_in_dim(attended, merged, start, 0)

    attended = lax.fori_loop(0, groups_here, group_step, jnp.zeros(layout, jnp.bfloat16))
    owners = attended.reshape(side, side, tok_rows, local_width)
    ahead_x = (offsets + place // side) % side
    ahead_y = (offsets + place % side) % side
    owners = owners[ahead_x][:, ahead_y]
    first = owners[:, :, :half].reshape(-1, local_width)
    second = jnp.swapaxes(owners[:, :, half:], 0, 1).reshape(-1, local_width)
    first = jnp.dot(first, output_weight, preferred_element_type=jnp.float32)
    second = jnp.dot(second, output_weight, preferred_element_type=jnp.float32)
    first = ring_reduce(first.reshape(side, side, half, width), side, True)
    second = ring_reduce(second.reshape(side, side, half, width), side, False)
    first = ring_reduce(first, side, False, False)
    second = ring_reduce(second, side, True, False)
    attention_update = jnp.concatenate([first, second], axis=0).astype(jnp.bfloat16)
    expert_input = rms_scale(
        residual_in.astype(jnp.float32) + attention_update.astype(jnp.float32), expert_gain
    )
    data_groups = lax.axis_size("dp")
    devices = data_groups * expert_groups
    hidden_split = FF // gate_weight.shape[2]
    experts = devices // hidden_split
    capacity = max(2, tok_rows * TOP * 3 // (2 * experts))
    chosen = expert_ids.reshape(-1)
    routes_here = chosen.shape[0]
    owners = jnp.arange(routes_here, dtype=jnp.int32) // TOP
    matches = (chosen[:, None] == jnp.arange(experts, dtype=jnp.int32)[None, :]).astype(jnp.int32)
    slots = jnp.sum((jnp.cumsum(matches, axis=0) - matches) * matches, axis=1)
    table = (
        jnp.full((experts * capacity,), tok_rows, jnp.int32)
        .at[chosen * capacity + slots]
        .set(owners)
    )
    lanes = 128
    sub = width // lanes
    tiles = expert_input.reshape(tok_rows, sub, lanes)
    padded = jnp.concatenate([tiles, jnp.zeros((1, sub, lanes), jnp.bfloat16)], axis=0)
    index = jnp.broadcast_to(
        table.reshape(experts, 1, capacity), (experts, hidden_split, capacity)
    ).reshape(-1)
    outgoing = padded[index].reshape(devices, capacity * sub, lanes)
    arrived = lax.all_to_all(outgoing, ("dp", "expert"), 0, 0, tiled=True)
    produced = expert_block(
        arrived.reshape(devices * capacity, sub, lanes), gate_weight, up_weight, down_weight
    )
    returned = lax.all_to_all(
        produced.reshape(devices, capacity * sub, lanes), ("dp", "expert"), 0, 0, tiled=True
    )
    pieces = returned.reshape(experts, hidden_split, capacity, sub, lanes)[chosen, :, slots]
    blended = jnp.sum(pieces.astype(jnp.float32), axis=1) * expert_mix.reshape(-1)[:, None, None]
    expert_update = (
        jnp.sum(blended.reshape(tok_rows, TOP, sub, lanes), axis=1)
        .reshape(tok_rows, width)
        .astype(jnp.bfloat16)
    )
    return (attention_update, expert_update)


def solution(mesh):
    in_specs = (
        P(("dp", "expert"), None),
        P(),
        P(None, "expert"),
        P(None, "expert"),
        P(None, "expert"),
        P("expert", None),
        P("dp", None, "expert"),
        P("dp", None, "expert"),
        P("dp", None),
        P("dp"),
        P("dp"),
        P(),
        P(("dp", "expert"), None),
        P(("dp", "expert"), None),
        P(("dp", "expert"), None, None),
        P(("dp", "expert"), None, None),
        P(("dp", "expert"), None, None),
    )
    out_specs = (P(("dp", "expert"), None), P(("dp", "expert"), None))
    return jax.shard_map(
        per_device, mesh=mesh, in_specs=in_specs, out_specs=out_specs, check_vma=False
    )
```
